32 devices in a mesh: dp: 8 (over z, x), tensor: 4 (over y, core).
Axes of the slice: x: 2, y: 2, z: 4, core: 2. Of those that a mesh axis runs over, the one named last changes fastest.
Arguments:
- tokens: bfloat16 [25088, 768], P(('dp', 'tensor')), may hold values from -6 to 6
- cotangent: bfloat16 [25088, 768], P(('dp', 'tensor')), may hold values from -6 to 6
- norm_gains: float32 [3, 768], replicated, may hold values from 0.5 to 1.5
- qkv_time: float32 [768, 3, 768], P('dp', None, 'tensor'), may hold values from -0.21875 to 0.21875
- proj_time: float32 [768, 768], P('tensor', 'dp'), may hold values from -0.625 to 0.625
- qkv_space: float32 [768, 3, 768], P('dp', None, 'tensor'), may hold values from -0.21875 to 0.21875
- proj_space: float32 [768, 768], P('tensor', 'dp'), may hold values from -1.75 to 1.75
- up_weight: float32 [768, 3072], P('dp', 'tensor'), may hold values from -0.21875 to 0.21875
- down_weight: float32 [3072, 768], P('tensor', 'dp'), may hold values from -0.109375 to 0.109375
Outputs:
- output: bfloat16 [25088, 768], P(('dp', 'tensor'))
- grad_tokens: float32 [25088, 768], P(('dp', 'tensor'))
- grad_gains: float32 [3, 768], replicated
- grad_qkv_time: float32 [768, 3, 768], P('dp', None, 'tensor')
- grad_proj_time: float32 [768, 768], P('tensor', 'dp')
- grad_qkv_space: float32 [768, 3, 768], P('dp', None, 'tensor')
- grad_proj_space: float32 [768, 768], P('tensor', 'dp')
- grad_up: float32 [768, 3072], P('dp', 'tensor')
- grad_down: float32 [3072, 768], P('tensor', 'dp')
The draws below stay inside these ranges and needn't reach their ends.
All inputs are finite; a program needn't handle non-finite values.
Results may differ from the reference program's by a relative error of at most 0.035.
Values may be sent and summed in bfloat16 or wider, within the bound.
No kernel may reach another device: no remote copies, remote signals or barrier semaphores. Data moves between devices by JAX's collectives and lax.ppermute only.
A program may use at most 192 MiB of HBM per device.

```python
import math
import jax
import jax.numpy as jnp
from jax import lax

D = 768
HEADS = 12
HD = 64
FF = 3072
FRAMES = 8
PATCH = 196
SEQ = 1568
CLIPS = 16
TOKENS = 25088


def with_spikes(entries, own_key, source, target, blocks, factor):
    owner, partner = [(jnp.arange(entries.shape[dim]) // (entries.shape[dim] // blocks)).reshape([-1 if axis == dim else 1 for axis in range(entries.ndim)]) for dim in (source, target)]
    chosen = jax.random.permutation(own_key, blocks)[partner]
    strong = (owner == chosen) | (owner == (partner + blocks // 2) % blocks)
    return jnp.where(strong, factor * entries, entries)


def levels(own_key, shape, shards, smallest, largest):
    def one(position, parts):
        steps = jax.random.uniform(jax.random.fold_in(jax.random.fold_in(own_key, 6), position), (parts,), jnp.float32, smallest / len(shards), largest / len(shards))
        return jnp.repeat(jnp.exp(steps), shape[position] // parts).reshape((-1,) + (1,) * (len(shape) - position - 1))

    gain = one(*shards[0])
    for cut in shards[1:]:
        gain = gain * one(*cut)
    return gain


def gaussian(rng, shape, scale, most, cuts=(), kind=jnp.bfloat16):
    drawn = jax.random.normal(rng, shape, jnp.float32) * scale
    if len(cuts) > 0:
        drawn = levels(rng, shape, cuts, -0.22, 0.18) * drawn
    return jnp.clip(drawn, min=-most, max=most).astype(kind)


def bell_draw_with(own_key, dims, width, limit, cuts, heavy, dtype=jnp.bfloat16):
    values = width * jax.random.normal(own_key, dims, jnp.float32)
    if cuts:
        values = values * levels(own_key, dims, cuts, -0.22, 0.18)
    return jnp.clip(with_spikes(values, jax.random.fold_in(own_key, 3), *heavy), -limit, limit).astype(dtype)


def setup_inputs(seed: int = 0) -> dict:
    splits = jax.random.split(jax.random.key(seed), 10)
    tokens = bell_draw_with(splits[0], (TOKENS, D), 1.0, 6.0, ((0, 32),), (0, 1, 32, 2.75))
    cotangent = bell_draw_with(splits[1], (TOKENS, D), 1.0, 6.0, ((0, 32),), (0, 1, 32, 2.75))
    norm_gains = jnp.clip(1.0 + 0.1 * jax.random.normal(splits[2], (3, D), jnp.float32), 0.5, 1.5)
    qkv_time = gaussian(splits[3], (D, 3, D), D ** -0.5, 0.21875, ((0, 8), (2, 4)), jnp.float32)
    proj_time = gaussian(splits[4], (D, D), (D // 8) ** -0.5, 0.625, ((0, 4), (1, 8)), jnp.float32)
    qkv_space = gaussian(splits[5], (D, 3, D), D ** -0.5, 0.21875, ((0, 8), (2, 4)), jnp.float32)
    proj_space = gaussian(splits[6], (D, D), (D // 64) ** -0.5, 1.75, ((0, 4), (1, 8)), jnp.float32)
    up_weight = gaussian(splits[7], (D, FF), D ** -0.5, 0.21875, ((0, 8), (1, 4)), jnp.float32)
    down_weight = gaussian(splits[8], (FF, D), FF ** -0.5, 0.109375, ((0, 4), (1, 8)), jnp.float32)
    return {"tokens": tokens, "cotangent": cotangent, "norm_gains": norm_gains, "qkv_time": qkv_time, "proj_time": proj_time, "qkv_space": qkv_space, "proj_space": proj_space, "up_weight": up_weight, "down_weight": down_weight}


@jax.custom_vjp
def low(v):
    return lax.optimization_barrier(v.astype(jnp.bfloat16)).astype(jnp.float32)

@jax.custom_vjp
def low_back(v):
    return v

def low_keep(v):
    return (low(v), None)

def low_pass(kept, grad):
    return (grad,)

def back_keep(v):
    return (v, None)

def back_low(kept, grad):
    return (low(grad),)
low.defvjp(low_keep, low_pass)
low_back.defvjp(back_keep, back_low)
epsilon = 1e-06
highest = lax.Precision.HIGHEST

def normalize(values, gain_row):
    center = values - lax.optimization_barrier(jnp.mean(values, axis=-1, keepdims=True))
    spread = lax.optimization_barrier(jnp.mean(center * center, axis=-1, keepdims=True))
    return center * lax.rsqrt(spread + epsilon) * gain_row

def attend(normed, w_qkv, w_proj, temporal):
    factor = 1.0 / math.sqrt(HD)
    mixed_qkv = jnp.dot(normed, w_qkv.reshape(D, 3 * D), precision=highest)
    mixed_qkv = low(low_back(mixed_qkv)).reshape(FRAMES, PATCH, 3, HEADS, HD)
    grouped = jnp.swapaxes(mixed_qkv, 0, 1) if temporal else mixed_qkv
    scores = jnp.einsum('blhe,bmhe->bhlm', grouped[:, :, 0], grouped[:, :, 1], precision=highest)
    scores = low_back(scores * factor)
    attn_probs = low(jax.nn.softmax(scores, axis=-1))
    attended = jnp.einsum('bhlm,bmhe->blhe', attn_probs, grouped[:, :, 2], precision=highest)
    if temporal:
        attended = jnp.swapaxes(attended, 0, 1)
    attended = low(low_back(attended.reshape(SEQ, D)))
    return low_back(jnp.dot(attended, w_proj, precision=highest))

def layer(clip_rows, norm_gains, qkv_time, proj_time, qkv_space, proj_space, up_weight, down_weight):
    normed = low(normalize(clip_rows, norm_gains[0]))
    after_time = clip_rows + attend(normed, qkv_time, proj_time, True)
    normed = low(normalize(after_time, norm_gains[1]))
    after_space = after_time + attend(normed, qkv_space, proj_space, False)
    normed = low(normalize(after_space, norm_gains[2]))
    hidden_pre = low_back(jnp.dot(normed, up_weight, precision=highest))
    hidden = low(jax.nn.gelu(hidden_pre, approximate=False))
    return after_space + low_back(jnp.dot(hidden, down_weight, precision=highest))

def reference(tokens, cotangent, norm_gains, qkv_time, proj_time, qkv_space, proj_space, up_weight, down_weight):
    checked = jax.checkpoint(layer)

    def whole(values, gain_rows, w_qt, w_pt, w_qs, w_ps, w_up, w_down):
        lowered = [low(w_qt), low(w_pt), low(w_qs), low(w_ps), low(w_up), low(w_down)]
        return lax.map(lambda clip_rows: checked(clip_rows, gain_rows, *lowered), values)
    values = tokens.astype(jnp.float32).reshape(CLIPS, SEQ, D)
    result, back_fn = jax.vjp(whole, values, norm_gains, qkv_time, proj_time, qkv_space, proj_space, up_weight, down_weight)
    grads = back_fn(cotangent.astype(jnp.float32).reshape(CLIPS, SEQ, D))
    output = result.reshape(TOKENS, D).astype(jnp.bfloat16)
    grad_tokens = grads[0].reshape(TOKENS, D)
    return (output, grad_tokens, grads[1], grads[2], grads[3], grads[4], grads[5], grads[6], grads[7])
```

```python
from functools import partial
import math

import jax
import jax.numpy as jnp
from jax import lax
from jax.sharding import Mesh, PartitionSpec as P

HD = 64
FRAMES = 8
PATCH = 196


epsilon = 1e-06


def normalize(values, gain_row):
    center = values - jnp.mean(values, axis=-1, keepdims=True)
    spread = jnp.mean(center * center, axis=-1, keepdims=True)
    return center * lax.rsqrt(spread + epsilon) * gain_row


def to_groups(values, temporal):
    trailing = values.shape[1:]
    if temporal:
        clip_count = values.shape[0] // (FRAMES * PATCH)
        shaped = values.reshape((clip_count, FRAMES, PATCH) + trailing)
        shaped = jnp.swapaxes(shaped, 1, 2)
        return shaped.reshape((clip_count * PATCH, FRAMES) + trailing)
    return values.reshape((-1, PATCH) + trailing)


def from_groups(values, temporal):
    trailing = values.shape[2:]
    if temporal:
        clip_count = values.shape[0] // PATCH
        values = jnp.swapaxes(values.reshape((clip_count, PATCH, FRAMES) + trailing), 1, 2)
    return values.reshape((-1,) + trailing)


def attend_forward(normed, w_qkv, temporal):
    factor = 1.0 / math.sqrt(HD)
    width_here = w_qkv.shape[2]
    mixed_qkv = jnp.dot(
        normed, w_qkv.reshape(w_qkv.shape[0], 3 * width_here), preferred_element_type=jnp.float32
    )
    mixed_qkv = mixed_qkv.astype(jnp.bfloat16).reshape(normed.shape[0], 3, width_here // HD, HD)
    grouped = to_groups(mixed_qkv, temporal)
    scores = (
        jnp.einsum(
            "blhe,bmhe->bhlm",
            grouped[:, :, 0],
            grouped[:, :, 1],
            preferred_element_type=jnp.float32,
        )
        * factor
    )
    row_top = jnp.max(scores, axis=-1, keepdims=True)
    shifted = jnp.exp(scores - row_top)
    row_total = jnp.sum(shifted, axis=-1, keepdims=True)
    attn_probs = (shifted / row_total).astype(jnp.bfloat16)
    attended = jnp.einsum(
        "bhlm,bmhe->blhe", attn_probs, grouped[:, :, 2], preferred_element_type=jnp.float32
    )
    merged = from_groups(attended.astype(jnp.bfloat16), temporal).reshape(
        normed.shape[0], width_here
    )
    return (grouped, row_top + jnp.log(row_total), merged)


def attend_backward(normed, w_qkv, w_proj, grouped, summary, merged, grad_rows, temporal):
    factor = 1.0 / math.sqrt(HD)
    width_here = merged.shape[1]
    grad_proj = jnp.dot(merged.T, grad_rows, preferred_element_type=jnp.float32)
    grad_merged = jnp.dot(grad_rows, w_proj.T, preferred_element_type=jnp.float32).astype(
        jnp.bfloat16
    )
    grad_attended = to_groups(grad_merged.reshape(normed.shape[0], width_here // HD, HD), temporal)
    query_rows = grouped[:, :, 0]
    key_rows = grouped[:, :, 1]
    value_rows = grouped[:, :, 2]
    scores = (
        jnp.einsum("blhe,bmhe->bhlm", query_rows, key_rows, preferred_element_type=jnp.float32)
        * factor
    )
    attn_probs = jnp.exp(scores - summary)
    grad_value = jnp.einsum(
        "bhlm,blhe->bmhe",
        attn_probs.astype(jnp.bfloat16),
        grad_attended,
        preferred_element_type=jnp.float32,
    )
    grad_probs = jnp.einsum(
        "blhe,bmhe->bhlm", grad_attended, value_rows, preferred_element_type=jnp.float32
    )
    grad_scores = attn_probs * (
        grad_probs - jnp.sum(grad_probs * attn_probs, axis=-1, keepdims=True)
    )
    grad_scores = grad_scores.astype(jnp.bfloat16)
    grad_query = (
        jnp.einsum("bhlm,bmhe->blhe", grad_scores, key_rows, preferred_element_type=jnp.float32)
        * factor
    )
    grad_key = (
        jnp.einsum("bhlm,blhe->bmhe", grad_scores, query_rows, preferred_element_type=jnp.float32)
        * factor
    )
    stacked = jnp.stack([grad_query, grad_key, grad_value], axis=2).astype(jnp.bfloat16)
    grad_mixed = from_groups(stacked, temporal).reshape(normed.shape[0], 3 * width_here)
    grad_qkv = jnp.dot(normed.T, grad_mixed, preferred_element_type=jnp.float32).reshape(
        normed.shape[1], 3, width_here
    )
    grad_normed = jnp.dot(
        grad_mixed,
        w_qkv.reshape(w_qkv.shape[0], 3 * width_here).T,
        preferred_element_type=jnp.float32,
    )
    return (grad_qkv, grad_proj, grad_normed)


WEIGHT_AXES = ("dp", "ty")


def gather_weights(shards, layouts):
    flat = [w.astype(jnp.bfloat16).reshape(1, -1) for w in shards]
    sizes = [f.shape[1] for f in flat]
    ny = lax.axis_size("ty")
    nd = lax.axis_size("dp")
    whole = lax.all_gather(jnp.concatenate(flat, axis=1), WEIGHT_AXES, axis=0, tiled=True)
    out = []
    offset = 0
    for w, size, (dp_dim, ty_dim) in zip(shards, sizes, layouts):
        part = whole[:, offset : offset + size].reshape((nd, ny) + w.shape)
        offset += size
        order = []
        for dim in range(w.ndim):
            if dim == dp_dim:
                order.append(0)
            if dim == ty_dim:
                order.append(1)
            order.append(dim + 2)
        shape = list(w.shape)
        shape[dp_dim] *= nd
        shape[ty_dim] *= ny
        out.append(jnp.transpose(part, order).reshape(shape))
    return out


def scatter_grads(grads, layouts, shard_shapes):
    ny = lax.axis_size("ty")
    nd = lax.axis_size("dp")
    flat = []
    for g, (dp_dim, ty_dim), shard in zip(grads, layouts, shard_shapes):
        split = []
        for dim in range(g.ndim):
            if dim == dp_dim:
                split.extend([nd, shard[dim]])
            elif dim == ty_dim:
                split.extend([ny, shard[dim]])
            else:
                split.append(shard[dim])
        parts = g.reshape(split)
        pos = 0
        ty_pos = dp_pos = None
        rest = []
        for dim in range(g.ndim):
            if dim == dp_dim:
                dp_pos = pos
                rest.append(pos + 1)
                pos += 2
            elif dim == ty_dim:
                ty_pos = pos
                rest.append(pos + 1)
                pos += 2
            else:
                rest.append(pos)
                pos += 1
        flat.append(jnp.transpose(parts, [dp_pos, ty_pos] + rest).reshape(ny * nd, -1))
    sizes = [f.shape[1] for f in flat]
    stacked = jnp.concatenate(flat, axis=1)
    width = stacked.shape[1]
    lane = 768 if width % 768 == 0 else width
    summed = lax.psum_scatter(
        stacked.reshape(ny * nd * (width // lane), lane),
        WEIGHT_AXES,
        scatter_dimension=0,
        tiled=True,
    ).reshape(-1)
    out = []
    offset = 0
    for size, shard in zip(sizes, shard_shapes):
        out.append(summed[offset : offset + size].reshape(shard))
        offset += size
    return out


def per_device(
    tokens,
    cotangent,
    norm_gains,
    qkv_time,
    proj_time,
    qkv_space,
    proj_space,
    up_weight,
    down_weight,
):
    qkv_layout = (0, 2)
    proj_layout = (1, 0)
    up_layout = (0, 1)
    down_layout = (1, 0)
    time_qkv, time_proj = gather_weights((qkv_time, proj_time), (qkv_layout, proj_layout))
    space_qkv, space_proj, up_full, down_full = gather_weights(
        (qkv_space, proj_space, up_weight, down_weight),
        (qkv_layout, proj_layout, up_layout, down_layout),
    )

    def spread_rows(values):
        return lax.all_gather(values, "core", axis=0, tiled=True)

    def sum_rows(values):
        return lax.psum_scatter(
            values.astype(jnp.bfloat16), "core", scatter_dimension=0, tiled=True
        ).astype(jnp.float32)

    spread_grads = spread_rows
    sum_grads = sum_rows

    inputs = tokens.astype(jnp.float32)
    normed_time = spread_rows(normalize(inputs, norm_gains[0]).astype(jnp.bfloat16))
    grouped_time, summary_time, merged_time = attend_forward(normed_time, time_qkv, True)
    after_time = inputs + sum_rows(
        jnp.dot(merged_time, time_proj, preferred_element_type=jnp.float32)
    )
    normed_space = spread_rows(normalize(after_time, norm_gains[1]).astype(jnp.bfloat16))
    grouped_space, summary_space, merged_space = attend_forward(normed_space, space_qkv, False)
    after_space = after_time + sum_rows(
        jnp.dot(merged_space, space_proj, preferred_element_type=jnp.float32)
    )
    normed_mlp = spread_rows(normalize(after_space, norm_gains[2]).astype(jnp.bfloat16))
    hidden_pre = jnp.dot(normed_mlp, up_full, preferred_element_type=jnp.float32)
    hidden = jax.nn.gelu(hidden_pre, approximate=False).astype(jnp.bfloat16)
    output = (
        after_space + sum_rows(jnp.dot(hidden, down_full, preferred_element_type=jnp.float32))
    ).astype(jnp.bfloat16)

    grad_after = cotangent.astype(jnp.float32)
    down_rows = spread_grads(grad_after.astype(jnp.bfloat16))
    grad_down = jnp.dot(hidden.T, down_rows, preferred_element_type=jnp.float32)
    grad_hidden = jnp.dot(down_rows, down_full.T, preferred_element_type=jnp.float32)
    _, gelu_back = jax.vjp(partial(jax.nn.gelu, approximate=False), hidden_pre)
    grad_pre = gelu_back(grad_hidden)[0].astype(jnp.bfloat16)
    grad_up = jnp.dot(normed_mlp.T, grad_pre, preferred_element_type=jnp.float32)
    grad_up, grad_down = scatter_grads(
        (grad_up, grad_down), (up_layout, down_layout), (up_weight.shape, down_weight.shape)
    )
    _, norm_back = jax.vjp(normalize, after_space, norm_gains[2])
    back_rows, gain_mlp = norm_back(
        sum_grads(jnp.dot(grad_pre, up_full.T, preferred_element_type=jnp.float32))
    )
    grad_after = grad_after + back_rows
    _, norm_back = jax.vjp(normalize, after_time, norm_gains[1])
    space_rows = spread_grads(grad_after.astype(jnp.bfloat16))
    grad_qkv_space, grad_proj_space, grad_normed = attend_backward(
        normed_space,
        space_qkv,
        space_proj,
        grouped_space,
        summary_space,
        merged_space,
        space_rows,
        False,
    )
    grad_qkv_space, grad_proj_space = scatter_grads(
        (grad_qkv_space, grad_proj_space),
        (qkv_layout, proj_layout),
        (qkv_space.shape, proj_space.shape),
    )
    back_rows, gain_space = norm_back(sum_grads(grad_normed))
    grad_after = grad_after + back_rows
    time_rows = spread_grads(grad_after.astype(jnp.bfloat16))
    grad_qkv_time, grad_proj_time, grad_normed = attend_backward(
        normed_time, time_qkv, time_proj, grouped_time, summary_time, merged_time, time_rows, True
    )
    grad_qkv_time, grad_proj_time = scatter_grads(
        (grad_qkv_time, grad_proj_time),
        (qkv_layout, proj_layout),
        (qkv_time.shape, proj_time.shape),
    )
    _, norm_back = jax.vjp(normalize, inputs, norm_gains[0])
    back_rows, gain_time = norm_back(sum_grads(grad_normed))
    grad_tokens = grad_after + back_rows
    grad_gains = lax.psum(jnp.stack([gain_time, gain_space, gain_mlp]), ("dp", "ty", "core"))
    return (
        output,
        grad_tokens,
        grad_gains,
        grad_qkv_time,
        grad_proj_time,
        grad_qkv_space,
        grad_proj_space,
        grad_up,
        grad_down,
    )


def solution(mesh):
    def run(*args):
        rows_here = args[0].shape[0] // mesh.size
        cores = FRAMES * PATCH // rows_here
        tensor = mesh.shape["tensor"]
        assert tensor % cores == 0
        devices = mesh.devices.reshape(mesh.shape["dp"], tensor // cores, cores)
        chips = Mesh(devices, ("dp", "ty", "core"))
        rows = P(("dp", "ty", "core"), None)
        qkv = P("dp", None, ("ty", "core"))
        proj = P(("ty", "core"), "dp")
        up = P("dp", ("ty", "core"))
        down = P(("ty", "core"), "dp")
        mapped = jax.shard_map(
            per_device,
            mesh=chips,
            in_specs=(rows, rows, P(), qkv, proj, qkv, proj, up, down),
            out_specs=(rows, rows, P(), qkv, proj, qkv, proj, up, down),
            check_vma=False,
        )
        return mapped(*args)

    return run
```

```python
from functools import partial
import math

import jax
import jax.numpy as jnp
from jax import lax
from jax.sharding import Mesh, PartitionSpec as P

HD = 64
FRAMES = 8
PATCH = 196


epsilon = 1e-06


def normalize(values, gain_row):
    center = values - jnp.mean(values, axis=-1, keepdims=True)
    spread = jnp.mean(center * center, axis=-1, keepdims=True)
    return center * lax.rsqrt(spread + epsilon) * gain_row


def to_groups(values, temporal):
    trailing = values.shape[1:]
    if temporal:
        clip_count = values.shape[0] // (FRAMES * PATCH)
        shaped = values.reshape((clip_count, FRAMES, PATCH) + trailing)
        shaped = jnp.swapaxes(shaped, 1, 2)
        return shaped.reshape((clip_count * PATCH, FRAMES) + trailing)
    return values.reshape((-1, PATCH) + trailing)


def from_groups(values, temporal):
    trailing = values.shape[2:]
    if temporal:
        clip_count = values.shape[0] // PATCH
        values = jnp.swapaxes(values.reshape((clip_count, PATCH, FRAMES) + trailing), 1, 2)
    return values.reshape((-1,) + trailing)


def attend_forward(normed, w_qkv, temporal):
    factor = 1.0 / math.sqrt(HD)
    width_here = w_qkv.shape[2]
    mixed_qkv = jnp.dot(
        normed, w_qkv.reshape(w_qkv.shape[0], 3 * width_here), preferred_element_type=jnp.float32
    )
    mixed_qkv = mixed_qkv.astype(jnp.bfloat16).reshape(normed.shape[0], 3, width_here // HD, HD)
    grouped = to_groups(mixed_qkv, temporal)
    scores = (
        jnp.einsum(
            "blhe,bmhe->bhlm",
            grouped[:, :, 0],
            grouped[:, :, 1],
            preferred_element_type=jnp.float32,
        )
        * factor
    )
    row_top = jnp.max(scores, axis=-1, keepdims=True)
    shifted = jnp.exp(scores - row_top)
    row_total = jnp.sum(shifted, axis=-1, keepdims=True)
    attn_probs = (shifted / row_total).astype(jnp.bfloat16)
    attended = jnp.einsum(
        "bhlm,bmhe->blhe", attn_probs, grouped[:, :, 2], preferred_element_type=jnp.float32
    )
    merged = from_groups(attended.astype(jnp.bfloat16), temporal).reshape(
        normed.shape[0], width_here
    )
    return (grouped, row_top + jnp.log(row_total), merged)


def attend_backward(normed, w_qkv, w_proj, grouped, summary, merged, grad_rows, temporal):
    factor = 1.0 / math.sqrt(HD)
    width_here = merged.shape[1]
    grad_proj = jnp.dot(merged.T, grad_rows, preferred_element_type=jnp.float32)
    grad_merged = jnp.dot(grad_rows, w_proj.T, preferred_element_type=jnp.float32).astype(
        jnp.bfloat16
    )
    grad_attended = to_groups(grad_merged.reshape(normed.shape[0], width_here // HD, HD), temporal)
    query_rows = grouped[:, :, 0]
    key_rows = grouped[:, :, 1]
    value_rows = grouped[:, :, 2]
    scores = (
        jnp.einsum("blhe,bmhe->bhlm", query_rows, key_rows, preferred_element_type=jnp.float32)
        * factor
    )
    attn_probs = jnp.exp(scores - summary)
    grad_value = jnp.einsum(
        "bhlm,blhe->bmhe",
        attn_probs.astype(jnp.bfloat16),
        grad_attended,
        preferred_element_type=jnp.float32,
    )
    grad_probs = jnp.einsum(
        "blhe,bmhe->bhlm", grad_attended, value_rows, preferred_element_type=jnp.float32
    )
    grad_scores = attn_probs * (
        grad_probs - jnp.sum(grad_probs * attn_probs, axis=-1, keepdims=True)
    )
    grad_scores = grad_scores.astype(jnp.bfloat16)
    grad_query = (
        jnp.einsum("bhlm,bmhe->blhe", grad_scores, key_rows, preferred_element_type=jnp.float32)
        * factor
    )
    grad_key = (
        jnp.einsum("bhlm,blhe->bmhe", grad_scores, query_rows, preferred_element_type=jnp.float32)
        * factor
    )
    stacked = jnp.stack([grad_query, grad_key, grad_value], axis=2).astype(jnp.bfloat16)
    grad_mixed = from_groups(stacked, temporal).reshape(normed.shape[0], 3 * width_here)
    grad_qkv = jnp.dot(normed.T, grad_mixed, preferred_element_type=jnp.float32).reshape(
        normed.shape[1], 3, width_here
    )
    grad_normed = jnp.dot(
        grad_mixed,
        w_qkv.reshape(w_qkv.shape[0], 3 * width_here).T,
        preferred_element_type=jnp.float32,
    )
    return (grad_qkv, grad_proj, grad_normed)


WEIGHT_AXES = ("dp", "ty")


def gather_weights(shards, layouts):
    flat = [w.astype(jnp.bfloat16).reshape(1, -1) for w in shards]
    sizes = [f.shape[1] for f in flat]
    ny = lax.axis_size("ty")
    nd = lax.axis_size("dp")
    whole = lax.all_gather(jnp.concatenate(flat, axis=1), WEIGHT_AXES, axis=0, tiled=True)
    out = []
    offset = 0
    for w, size, (dp_dim, ty_dim) in zip(shards, sizes, layouts):
        part = whole[:, offset : offset + size].reshape((nd, ny) + w.shape)
        offset += size
        order = []
        for dim in range(w.ndim):
            if dim == dp_dim:
                order.append(0)
            if dim == ty_dim:
                order.append(1)
            order.append(dim + 2)
        shape = list(w.shape)
        shape[dp_dim] *= nd
        shape[ty_dim] *= ny
        out.append(jnp.transpose(part, order).reshape(shape))
    return out


def scatter_grads(grads, layouts, shard_shapes):
    ny = lax.axis_size("ty")
    nd = lax.axis_size("dp")
    flat = []
    for g, (dp_dim, ty_dim), shard in zip(grads, layouts, shard_shapes):
        split = []
        for dim in range(g.ndim):
            if dim == dp_dim:
                split.extend([nd, shard[dim]])
            elif dim == ty_dim:
                split.extend([ny, shard[dim]])
            else:
                split.append(shard[dim])
        parts = g.reshape(split)
        pos = 0
        ty_pos = dp_pos = None
        rest = []
        for dim in range(g.ndim):
            if dim == dp_dim:
                dp_pos = pos
                rest.append(pos + 1)
                pos += 2
            elif dim == ty_dim:
                ty_pos = pos
                rest.append(pos + 1)
                pos += 2
            else:
                rest.append(pos)
                pos += 1
        flat.append(
            jnp.transpose(parts, [dp_pos, ty_pos] + rest).reshape(ny * nd, -1).astype(jnp.bfloat16)
        )
    sizes = [f.shape[1] for f in flat]
    stacked = jnp.concatenate(flat, axis=1)
    width = stacked.shape[1]
    lane = 768 if width % 768 == 0 else width
    summed = lax.psum_scatter(
        stacked.reshape(ny * nd * (width // lane), lane),
        WEIGHT_AXES,
        scatter_dimension=0,
        tiled=True,
    ).reshape(-1)
    out = []
    offset = 0
    for size, shard in zip(sizes, shard_shapes):
        out.append(summed[offset : offset + size].reshape(shard).astype(jnp.float32))
        offset += size
    return out


def per_device(
    tokens,
    cotangent,
    norm_gains,
    qkv_time,
    proj_time,
    qkv_space,
    proj_space,
    up_weight,
    down_weight,
):
    qkv_layout = (0, 2)
    proj_layout = (1, 0)
    up_layout = (0, 1)
    down_layout = (1, 0)
    time_qkv, time_proj = gather_weights((qkv_time, proj_time), (qkv_layout, proj_layout))
    space_qkv, space_proj = gather_weights((qkv_space, proj_space), (qkv_layout, proj_layout))
    up_full, down_full = gather_weights((up_weight, down_weight), (up_layout, down_layout))

    def swap(values):
        return lax.ppermute(values, "core", perm=[(0, 1), (1, 0)])

    def spread_rows(values):
        return jnp.concatenate([values, swap(values)], axis=0)

    def sum_rows(values):
        half = values.shape[0] // 2
        return values[:half] + swap(values[half:].astype(jnp.bfloat16)).astype(jnp.float32)

    spread_grads = spread_rows
    sum_grads = sum_rows

    inputs = tokens.astype(jnp.float32)
    normed_time = spread_rows(normalize(inputs, norm_gains[0]).astype(jnp.bfloat16))
    grouped_time, summary_time, merged_time = attend_forward(normed_time, time_qkv, True)
    after_time = inputs + sum_rows(
        jnp.dot(merged_time, time_proj, preferred_element_type=jnp.float32)
    )
    normed_space = spread_rows(normalize(after_time, norm_gains[1]).astype(jnp.bfloat16))
    grouped_space, summary_space, merged_space = attend_forward(normed_space, space_qkv, False)
    after_space = after_time + sum_rows(
        jnp.dot(merged_space, space_proj, preferred_element_type=jnp.float32)
    )
    normed_mlp = spread_rows(normalize(after_space, norm_gains[2]).astype(jnp.bfloat16))
    hidden_pre = jnp.dot(normed_mlp, up_full, preferred_element_type=jnp.float32)
    hidden = jax.nn.gelu(hidden_pre, approximate=False).astype(jnp.bfloat16)
    output = (
        after_space + sum_rows(jnp.dot(hidden, down_full, preferred_element_type=jnp.float32))
    ).astype(jnp.bfloat16)

    grad_after = cotangent.astype(jnp.float32)
    down_rows = spread_grads(grad_after.astype(jnp.bfloat16))
    grad_down = jnp.dot(hidden.T, down_rows, preferred_element_type=jnp.float32)
    grad_hidden = jnp.dot(down_rows, down_full.T, preferred_element_type=jnp.float32)
    _, gelu_back = jax.vjp(partial(jax.nn.gelu, approximate=False), hidden_pre)
    grad_pre = gelu_back(grad_hidden)[0].astype(jnp.bfloat16)
    grad_up = jnp.dot(normed_mlp.T, grad_pre, preferred_element_type=jnp.float32)
    grad_up, grad_down = scatter_grads(
        (grad_up, grad_down), (up_layout, down_layout), (up_weight.shape, down_weight.shape)
    )
    _, norm_back = jax.vjp(normalize, after_space, norm_gains[2])
    back_rows, gain_mlp = norm_back(
        sum_grads(jnp.dot(grad_pre, up_full.T, preferred_element_type=jnp.float32))
    )
    grad_after = grad_after + back_rows
    _, norm_back = jax.vjp(normalize, after_time, norm_gains[1])
    space_rows = spread_grads(grad_after.astype(jnp.bfloat16))
    grad_qkv_space, grad_proj_space, grad_normed = attend_backward(
        normed_space,
        space_qkv,
        space_proj,
        grouped_space,
        summary_space,
        merged_space,
        space_rows,
        False,
    )
    grad_qkv_space, grad_proj_space = scatter_grads(
        (grad_qkv_space, grad_proj_space),
        (qkv_layout, proj_layout),
        (qkv_space.shape, proj_space.shape),
    )
    back_rows, gain_space = norm_back(sum_grads(grad_normed))
    grad_after = grad_after + back_rows
    time_rows = spread_grads(grad_after.astype(jnp.bfloat16))
    grad_qkv_time, grad_proj_time, grad_normed = attend_backward(
        normed_time, time_qkv, time_proj, grouped_time, summary_time, merged_time, time_rows, True
    )
    grad_qkv_time, grad_proj_time = scatter_grads(
        (grad_qkv_time, grad_proj_time),
        (qkv_layout, proj_layout),
        (qkv_time.shape, proj_time.shape),
    )
    _, norm_back = jax.vjp(normalize, inputs, norm_gains[0])
    back_rows, gain_time = norm_back(sum_grads(grad_normed))
    grad_tokens = grad_after + back_rows
    grad_gains = lax.psum(jnp.stack([gain_time, gain_space, gain_mlp]), ("dp", "ty", "core"))
    return (
        output,
        grad_tokens,
        grad_gains,
        grad_qkv_time,
        grad_proj_time,
        grad_qkv_space,
        grad_proj_space,
        grad_up,
        grad_down,
    )


def solution(mesh):
    def run(*args):
        rows_here = args[0].shape[0] // mesh.size
        cores = FRAMES * PATCH // rows_here
        tensor = mesh.shape["tensor"]
        assert tensor % cores == 0
        devices = mesh.devices.reshape(mesh.shape["dp"], tensor // cores, cores)
        chips = Mesh(devices, ("dp", "ty", "core"))
        rows = P(("dp", "ty", "core"), None)
        qkv = P("dp", None, ("ty", "core"))
        proj = P(("ty", "core"), "dp")
        up = P("dp", ("ty", "core"))
        down = P(("ty", "core"), "dp")
        mapped = jax.shard_map(
            per_device,
            mesh=chips,
            in_specs=(rows, rows, P(), qkv, proj, qkv, proj, up, down),
            out_specs=(rows, rows, P(), qkv, proj, qkv, proj, up, down),
            check_vma=False,
        )
        return mapped(*args)

    return run
```

```python
from functools import partial
import math

import jax
import jax.numpy as jnp
from jax import lax
from jax.sharding import Mesh, PartitionSpec as P


HD = 64
FRAMES = 8
PATCH = 196


epsilon = 1e-06


def normalize(values, gain_row):
    center = values - jnp.mean(values, axis=-1, keepdims=True)
    spread = jnp.mean(center * center, axis=-1, keepdims=True)
    return center * lax.rsqrt(spread + epsilon) * gain_row


def to_groups(values, temporal):
    trailing = values.shape[1:]
    if temporal:
        clip_count = values.shape[0] // (FRAMES * PATCH)
        shaped = values.reshape((clip_count, FRAMES, PATCH) + trailing)
        shaped = jnp.swapaxes(shaped, 1, 2)
        return shaped.reshape((clip_count * PATCH, FRAMES) + trailing)
    return values.reshape((-1, PATCH) + trailing)


def from_groups(values, temporal):
    trailing = values.shape[2:]
    if temporal:
        clip_count = values.shape[0] // PATCH
        values = jnp.swapaxes(values.reshape((clip_count, PATCH, FRAMES) + trailing), 1, 2)
    return values.reshape((-1,) + trailing)


def attend_forward(normed, w_qkv, temporal):
    factor = 1.0 / math.sqrt(HD)
    width_here = w_qkv.shape[2]
    mixed_qkv = jnp.dot(
        normed, w_qkv.reshape(w_qkv.shape[0], 3 * width_here), preferred_element_type=jnp.float32
    )
    mixed_qkv = mixed_qkv.astype(jnp.bfloat16).reshape(normed.shape[0], 3, width_here // HD, HD)
    grouped = to_groups(mixed_qkv, temporal)
    scores = (
        jnp.einsum(
            "blhe,bmhe->bhlm",
            grouped[:, :, 0],
            grouped[:, :, 1],
            preferred_element_type=jnp.float32,
        )
        * factor
    )
    row_top = jnp.max(scores, axis=-1, keepdims=True)
    shifted = jnp.exp(scores - row_top)
    row_total = jnp.sum(shifted, axis=-1, keepdims=True)
    attn_probs = (shifted / row_total).astype(jnp.bfloat16)
    attended = jnp.einsum(
        "bhlm,bmhe->blhe", attn_probs, grouped[:, :, 2], preferred_element_type=jnp.float32
    )
    merged = from_groups(attended.astype(jnp.bfloat16), temporal).reshape(
        normed.shape[0], width_here
    )
    return (grouped, row_top + jnp.log(row_total), merged)


def attend_backward(normed, w_qkv, w_proj, grouped, summary, merged, grad_rows, temporal):
    factor = 1.0 / math.sqrt(HD)
    width_here = merged.shape[1]
    grad_proj = jnp.dot(merged.T, grad_rows, preferred_element_type=jnp.float32)
    grad_merged = jnp.dot(grad_rows, w_proj.T, preferred_element_type=jnp.float32).astype(
        jnp.bfloat16
    )
    grad_attended = to_groups(grad_merged.reshape(normed.shape[0], width_here // HD, HD), temporal)
    query_rows = grouped[:, :, 0]
    key_rows = grouped[:, :, 1]
    value_rows = grouped[:, :, 2]
    scores = (
        jnp.einsum("blhe,bmhe->bhlm", query_rows, key_rows, preferred_element_type=jnp.float32)
        * factor
    )
    attn_probs = jnp.exp(scores - summary)
    grad_value = jnp.einsum(
        "bhlm,blhe->bmhe",
        attn_probs.astype(jnp.bfloat16),
        grad_attended,
        preferred_element_type=jnp.float32,
    )
    grad_probs = jnp.einsum(
        "blhe,bmhe->bhlm", grad_attended, value_rows, preferred_element_type=jnp.float32
    )
    grad_scores = attn_probs * (
        grad_probs - jnp.sum(grad_probs * attn_probs, axis=-1, keepdims=True)
    )
    grad_scores = grad_scores.astype(jnp.bfloat16)
    grad_query = (
        jnp.einsum("bhlm,bmhe->blhe", grad_scores, key_rows, preferred_element_type=jnp.float32)
        * factor
    )
    grad_key = (
        jnp.einsum("bhlm,blhe->bmhe", grad_scores, query_rows, preferred_element_type=jnp.float32)
        * factor
    )
    stacked = jnp.stack([grad_query, grad_key, grad_value], axis=2).astype(jnp.bfloat16)
    grad_mixed = from_groups(stacked, temporal).reshape(normed.shape[0], 3 * width_here)
    grad_qkv = jnp.dot(normed.T, grad_mixed, preferred_element_type=jnp.float32).reshape(
        normed.shape[1], 3, width_here
    )
    grad_normed = jnp.dot(
        grad_mixed,
        w_qkv.reshape(w_qkv.shape[0], 3 * width_here).T,
        preferred_element_type=jnp.float32,
    )
    return (grad_qkv, grad_proj, grad_normed)


def swap_ty(values):
    return lax.ppermute(values, "ty", perm=[(0, 1), (1, 0)])


def gather_weights(shards, layouts):
    assert lax.axis_size("ty") == 2
    flat = [w.astype(jnp.bfloat16).reshape(1, -1) for w in shards]
    sizes = [f.shape[1] for f in flat]
    nd = lax.axis_size("dp")
    mine = lax.all_gather(jnp.concatenate(flat, axis=1), "dp", axis=0, tiled=True)
    whole = jnp.stack([mine, swap_ty(mine)])
    out = []
    offset = 0
    for w, size, (dp_dim, ty_dim) in zip(shards, sizes, layouts):
        part = whole[:, :, offset : offset + size].reshape((2, nd) + w.shape)
        offset += size
        order = []
        for dim in range(w.ndim):
            if dim == dp_dim:
                order.append(1)
            if dim == ty_dim:
                order.append(0)
            order.append(dim + 2)
        shape = list(w.shape)
        shape[dp_dim] *= nd
        shape[ty_dim] *= 2
        out.append(jnp.transpose(part, order).reshape(shape))
    return out


def scatter_grads(grads, layouts, shard_shapes):
    nd = lax.axis_size("dp")
    flat = []
    for g, (dp_dim, ty_dim), shard in zip(grads, layouts, shard_shapes):
        split = []
        for dim in range(g.ndim):
            if dim == dp_dim:
                split.extend([nd, shard[dim]])
            elif dim == ty_dim:
                split.extend([2, shard[dim]])
            else:
                split.append(shard[dim])
        parts = g.reshape(split)
        pos = 0
        ty_pos = dp_pos = None
        rest = []
        for dim in range(g.ndim):
            if dim == dp_dim:
                dp_pos = pos
                rest.append(pos + 1)
                pos += 2
            elif dim == ty_dim:
                ty_pos = pos
                rest.append(pos + 1)
                pos += 2
            else:
                rest.append(pos)
                pos += 1
        flat.append(jnp.transpose(parts, [ty_pos, dp_pos] + rest).reshape(2, nd, -1))
    sizes = [f.shape[2] for f in flat]
    stacked = jnp.concatenate(flat, axis=2)
    own = stacked[0] + swap_ty(stacked[1].astype(jnp.bfloat16)).astype(jnp.float32)
    width = own.shape[1]
    lane = 768 if width % 768 == 0 else width
    summed = lax.psum_scatter(
        own.astype(jnp.bfloat16).reshape(-1, lane), "dp", scatter_dimension=0, tiled=True
    ).reshape(-1)
    out = []
    offset = 0
    for size, shard in zip(sizes, shard_shapes):
        out.append(summed[offset : offset + size].reshape(shard).astype(jnp.float32))
        offset += size
    return out


def per_device(
    tokens,
    cotangent,
    norm_gains,
    qkv_time,
    proj_time,
    qkv_space,
    proj_space,
    up_weight,
    down_weight,
):
    qkv_layout = (0, 2)
    proj_layout = (1, 0)
    up_layout = (0, 1)
    down_layout = (1, 0)
    time_qkv, time_proj = gather_weights((qkv_time, proj_time), (qkv_layout, proj_layout))
    space_qkv, space_proj = gather_weights((qkv_space, proj_space), (qkv_layout, proj_layout))
    up_full, down_full = gather_weights((up_weight, down_weight), (up_layout, down_layout))

    def swap(values):
        return lax.ppermute(values, "core", perm=[(0, 1), (1, 0)])

    def spread_rows(values):
        return jnp.concatenate([values, swap(values)], axis=0)

    def sum_rows(values):
        half = values.shape[0] // 2
        return values[:half] + swap(values[half:].astype(jnp.bfloat16)).astype(jnp.float32)

    spread_grads = spread_rows
    sum_grads = sum_rows

    inputs = tokens.astype(jnp.float32)
    normed_time = spread_rows(normalize(inputs, norm_gains[0]).astype(jnp.bfloat16))
    grouped_time, summary_time, merged_time = attend_forward(normed_time, time_qkv, True)
    after_time = inputs + sum_rows(
        jnp.dot(merged_time, time_proj, preferred_element_type=jnp.float32)
    )
    normed_space = spread_rows(normalize(after_time, norm_gains[1]).astype(jnp.bfloat16))
    grouped_space, summary_space, merged_space = attend_forward(normed_space, space_qkv, False)
    after_space = after_time + sum_rows(
        jnp.dot(merged_space, space_proj, preferred_element_type=jnp.float32)
    )
    normed_mlp = spread_rows(normalize(after_space, norm_gains[2]).astype(jnp.bfloat16))
    hidden_pre = jnp.dot(normed_mlp, up_full, preferred_element_type=jnp.float32)
    hidden = jax.nn.gelu(hidden_pre, approximate=False).astype(jnp.bfloat16)
    output = (
        after_space + sum_rows(jnp.dot(hidden, down_full, preferred_element_type=jnp.float32))
    ).astype(jnp.bfloat16)

    grad_after = cotangent.astype(jnp.float32)
    down_rows = spread_grads(grad_after.astype(jnp.bfloat16))
    grad_down = jnp.dot(hidden.T, down_rows, preferred_element_type=jnp.float32)
    grad_hidden = jnp.dot(down_rows, down_full.T, preferred_element_type=jnp.float32)
    _, gelu_back = jax.vjp(partial(jax.nn.gelu, approximate=False), hidden_pre)
    grad_pre = gelu_back(grad_hidden)[0].astype(jnp.bfloat16)
    grad_up = jnp.dot(normed_mlp.T, grad_pre, preferred_element_type=jnp.float32)
    grad_up, grad_down = scatter_grads(
        (grad_up, grad_down), (up_layout, down_layout), (up_weight.shape, down_weight.shape)
    )
    _, norm_back = jax.vjp(normalize, after_space, norm_gains[2])
    back_rows, gain_mlp = norm_back(
        sum_grads(jnp.dot(grad_pre, up_full.T, preferred_element_type=jnp.float32))
    )
    grad_after = grad_after + back_rows
    _, norm_back = jax.vjp(normalize, after_time, norm_gains[1])
    space_rows = spread_grads(grad_after.astype(jnp.bfloat16))
    grad_qkv_space, grad_proj_space, grad_normed = attend_backward(
        normed_space,
        space_qkv,
        space_proj,
        grouped_space,
        summary_space,
        merged_space,
        space_rows,
        False,
    )
    grad_qkv_space, grad_proj_space = scatter_grads(
        (grad_qkv_space, grad_proj_space),
        (qkv_layout, proj_layout),
        (qkv_space.shape, proj_space.shape),
    )
    back_rows, gain_space = norm_back(sum_grads(grad_normed))
    grad_after = grad_after + back_rows
    time_rows = spread_grads(grad_after.astype(jnp.bfloat16))
    grad_qkv_time, grad_proj_time, grad_normed = attend_backward(
        normed_time, time_qkv, time_proj, grouped_time, summary_time, merged_time, time_rows, True
    )
    grad_qkv_time, grad_proj_time = scatter_grads(
        (grad_qkv_time, grad_proj_time),
        (qkv_layout, proj_layout),
        (qkv_time.shape, proj_time.shape),
    )
    _, norm_back = jax.vjp(normalize, inputs, norm_gains[0])
    back_rows, gain_time = norm_back(sum_grads(grad_normed))
    grad_tokens = grad_after + back_rows
    grad_gains = lax.psum(jnp.stack([gain_time, gain_space, gain_mlp]), ("dp", "ty", "core"))
    return (
        output,
        grad_tokens,
        grad_gains,
        grad_qkv_time,
        grad_proj_time,
        grad_qkv_space,
        grad_proj_space,
        grad_up,
        grad_down,
    )


def solution(mesh):
    def run(*args):
        rows_here = args[0].shape[0] // mesh.size
        cores = FRAMES * PATCH // rows_here
        tensor = mesh.shape["tensor"]
        assert tensor % cores == 0
        devices = mesh.devices.reshape(mesh.shape["dp"], tensor // cores, cores)
        chips = Mesh(devices, ("dp", "ty", "core"))
        rows = P(("dp", "ty", "core"), None)
        qkv = P("dp", None, ("ty", "core"))
        proj = P(("ty", "core"), "dp")
        up = P("dp", ("ty", "core"))
        down = P(("ty", "core"), "dp")
        mapped = jax.shard_map(
            per_device,
            mesh=chips,
            in_specs=(rows, rows, P(), qkv, proj, qkv, proj, up, down),
            out_specs=(rows, rows, P(), qkv, proj, qkv, proj, up, down),
            check_vma=False,
        )
        return mapped(*args)

    return run
```

```python
from functools import partial
import math

import jax
import jax.numpy as jnp
from jax import lax
from jax.sharding import Mesh, PartitionSpec as P


HD = 64
FRAMES = 8
PATCH = 196


epsilon = 1e-06


def normalize(values, gain_row):
    center = values - jnp.mean(values, axis=-1, keepdims=True)
    spread = jnp.mean(center * center, axis=-1, keepdims=True)
    return center * lax.rsqrt(spread + epsilon) * gain_row


def to_groups(values, temporal):
    trailing = values.shape[1:]
    if temporal:
        clip_count = values.shape[0] // (FRAMES * PATCH)
        shaped = values.reshape((clip_count, FRAMES, PATCH) + trailing)
        shaped = jnp.swapaxes(shaped, 1, 2)
        return shaped.reshape((clip_count * PATCH, FRAMES) + trailing)
    return values.reshape((-1, PATCH) + trailing)


def from_groups(values, temporal):
    trailing = values.shape[2:]
    if temporal:
        clip_count = values.shape[0] // PATCH
        values = jnp.swapaxes(values.reshape((clip_count, PATCH, FRAMES) + trailing), 1, 2)
    return values.reshape((-1,) + trailing)


def attend_forward(normed, w_qkv, temporal):
    factor = 1.0 / math.sqrt(HD)
    width_here = w_qkv.shape[2]
    mixed_qkv = jnp.dot(
        normed, w_qkv.reshape(w_qkv.shape[0], 3 * width_here), preferred_element_type=jnp.float32
    )
    mixed_qkv = mixed_qkv.astype(jnp.bfloat16).reshape(normed.shape[0], 3, width_here // HD, HD)
    grouped = to_groups(mixed_qkv, temporal)
    scores = (
        jnp.einsum(
            "blhe,bmhe->bhlm",
            grouped[:, :, 0],
            grouped[:, :, 1],
            preferred_element_type=jnp.float32,
        )
        * factor
    )
    row_top = jnp.max(scores, axis=-1, keepdims=True)
    shifted = jnp.exp(scores - row_top)
    row_total = jnp.sum(shifted, axis=-1, keepdims=True)
    attn_probs = (shifted / row_total).astype(jnp.bfloat16)
    attended = jnp.einsum(
        "bhlm,bmhe->blhe", attn_probs, grouped[:, :, 2], preferred_element_type=jnp.float32
    )
    merged = from_groups(attended.astype(jnp.bfloat16), temporal).reshape(
        normed.shape[0], width_here
    )
    return (grouped, row_top + jnp.log(row_total), merged)


def attend_backward(normed, w_qkv, w_proj, grouped, summary, merged, grad_rows, temporal):
    factor = 1.0 / math.sqrt(HD)
    width_here = merged.shape[1]
    grad_proj = jnp.dot(merged.T, grad_rows, preferred_element_type=jnp.float32)
    grad_merged = jnp.dot(grad_rows, w_proj.T, preferred_element_type=jnp.float32).astype(
        jnp.bfloat16
    )
    grad_attended = to_groups(grad_merged.reshape(normed.shape[0], width_here // HD, HD), temporal)
    query_rows = grouped[:, :, 0]
    key_rows = grouped[:, :, 1]
    value_rows = grouped[:, :, 2]
    scores = (
        jnp.einsum("blhe,bmhe->bhlm", query_rows, key_rows, preferred_element_type=jnp.float32)
        * factor
    )
    attn_probs = jnp.exp(scores - summary)
    grad_value = jnp.einsum(
        "bhlm,blhe->bmhe",
        attn_probs.astype(jnp.bfloat16),
        grad_attended,
        preferred_element_type=jnp.float32,
    )
    grad_probs = jnp.einsum(
        "blhe,bmhe->bhlm", grad_attended, value_rows, preferred_element_type=jnp.float32
    )
    grad_scores = attn_probs * (
        grad_probs - jnp.sum(grad_probs * attn_probs, axis=-1, keepdims=True)
    )
    grad_scores = grad_scores.astype(jnp.bfloat16)
    grad_query = (
        jnp.einsum("bhlm,bmhe->blhe", grad_scores, key_rows, preferred_element_type=jnp.float32)
        * factor
    )
    grad_key = (
        jnp.einsum("bhlm,blhe->bmhe", grad_scores, query_rows, preferred_element_type=jnp.float32)
        * factor
    )
    stacked = jnp.stack([grad_query, grad_key, grad_value], axis=2).astype(jnp.bfloat16)
    grad_mixed = from_groups(stacked, temporal).reshape(normed.shape[0], 3 * width_here)
    grad_qkv = jnp.dot(normed.T, grad_mixed, preferred_element_type=jnp.float32).reshape(
        normed.shape[1], 3, width_here
    )
    grad_normed = jnp.dot(
        grad_mixed,
        w_qkv.reshape(w_qkv.shape[0], 3 * width_here).T,
        preferred_element_type=jnp.float32,
    )
    return (grad_qkv, grad_proj, grad_normed)


WEIGHT_AXES = ("dp", "ty")


def gather_weights(shards, layouts):
    flat = [w.astype(jnp.bfloat16).reshape(1, -1) for w in shards]
    sizes = [f.shape[1] for f in flat]
    ny = lax.axis_size("ty")
    nd = lax.axis_size("dp")
    whole = lax.all_gather(jnp.concatenate(flat, axis=1), WEIGHT_AXES, axis=0, tiled=True)
    out = []
    offset = 0
    for w, size, (dp_dim, ty_dim) in zip(shards, sizes, layouts):
        part = whole[:, offset : offset + size].reshape((nd, ny) + w.shape)
        offset += size
        order = []
        for dim in range(w.ndim):
            if dim == dp_dim:
                order.append(0)
            if dim == ty_dim:
                order.append(1)
            order.append(dim + 2)
        shape = list(w.shape)
        shape[dp_dim] *= nd
        shape[ty_dim] *= ny
        out.append(jnp.transpose(part, order).reshape(shape))
    return out


def scatter_grads(grads, layouts, shard_shapes):
    ny = lax.axis_size("ty")
    nd = lax.axis_size("dp")
    assert ny == 2
    flat = []
    for g, (dp_dim, ty_dim), shard in zip(grads, layouts, shard_shapes):
        split = []
        for dim in range(g.ndim):
            if dim == dp_dim:
                split.extend([nd, shard[dim]])
            elif dim == ty_dim:
                split.extend([ny, shard[dim]])
            else:
                split.append(shard[dim])
        parts = g.reshape(split)
        pos = 0
        ty_pos = dp_pos = None
        rest = []
        for dim in range(g.ndim):
            if dim == dp_dim:
                dp_pos = pos
                rest.append(pos + 1)
                pos += 2
            elif dim == ty_dim:
                ty_pos = pos
                rest.append(pos + 1)
                pos += 2
            else:
                rest.append(pos)
                pos += 1
        flat.append(
            jnp.transpose(parts, [dp_pos, ty_pos] + rest)
            .reshape(nd, ny, -1)
            .astype(jnp.bfloat16)
        )
    sizes = [f.shape[2] for f in flat]
    stacked = jnp.concatenate(flat, axis=2)
    width = stacked.shape[2]
    lane = 768 if width % 768 == 0 else width
    blocks = lax.psum_scatter(
        stacked.reshape(-1, lane), "dp", scatter_dimension=0, tiled=True
    ).reshape(ny, width)
    return blocks, sizes, shard_shapes


def finish_grads(blocks, sizes, shard_shapes):
    here = lax.axis_index("ty")
    own = lax.dynamic_index_in_dim(blocks, here, axis=0, keepdims=False)
    other = lax.dynamic_index_in_dim(blocks, 1 - here, axis=0, keepdims=False)
    summed = own.astype(jnp.float32) + swap_ty(other).astype(jnp.float32)
    out = []
    offset = 0
    for size, shard in zip(sizes, shard_shapes):
        out.append(summed[offset : offset + size].reshape(shard))
        offset += size
    return out


def swap_ty(values):
    return lax.ppermute(values, "ty", perm=[(0, 1), (1, 0)])


def per_device(
    tokens,
    cotangent,
    norm_gains,
    qkv_time,
    proj_time,
    qkv_space,
    proj_space,
    up_weight,
    down_weight,
):
    qkv_layout = (0, 2)
    proj_layout = (1, 0)
    up_layout = (0, 1)
    down_layout = (1, 0)
    time_qkv, time_proj = gather_weights((qkv_time, proj_time), (qkv_layout, proj_layout))
    space_qkv, space_proj = gather_weights((qkv_space, proj_space), (qkv_layout, proj_layout))
    up_full, down_full = gather_weights((up_weight, down_weight), (up_layout, down_layout))

    def swap(values):
        return lax.ppermute(values, "core", perm=[(0, 1), (1, 0)])

    def spread_rows(values):
        return jnp.concatenate([values, swap(values)], axis=0)

    def sum_rows(values):
        half = values.shape[0] // 2
        return values[:half] + swap(values[half:].astype(jnp.bfloat16)).astype(jnp.float32)

    spread_grads = spread_rows
    sum_grads = sum_rows

    inputs = tokens.astype(jnp.float32)
    normed_time = spread_rows(normalize(inputs, norm_gains[0]).astype(jnp.bfloat16))
    grouped_time, summary_time, merged_time = attend_forward(normed_time, time_qkv, True)
    after_time = inputs + sum_rows(
        jnp.dot(merged_time, time_proj, preferred_element_type=jnp.float32)
    )
    normed_space = spread_rows(normalize(after_time, norm_gains[1]).astype(jnp.bfloat16))
    grouped_space, summary_space, merged_space = attend_forward(normed_space, space_qkv, False)
    after_space = after_time + sum_rows(
        jnp.dot(merged_space, space_proj, preferred_element_type=jnp.float32)
    )
    normed_mlp = spread_rows(normalize(after_space, norm_gains[2]).astype(jnp.bfloat16))
    hidden_pre = jnp.dot(normed_mlp, up_full, preferred_element_type=jnp.float32)
    hidden = jax.nn.gelu(hidden_pre, approximate=False).astype(jnp.bfloat16)
    output = (
        after_space + sum_rows(jnp.dot(hidden, down_full, preferred_element_type=jnp.float32))
    ).astype(jnp.bfloat16)

    grad_after = cotangent.astype(jnp.float32)
    down_rows = spread_grads(grad_after.astype(jnp.bfloat16))
    grad_down = jnp.dot(hidden.T, down_rows, preferred_element_type=jnp.float32)
    grad_hidden = jnp.dot(down_rows, down_full.T, preferred_element_type=jnp.float32)
    _, gelu_back = jax.vjp(partial(jax.nn.gelu, approximate=False), hidden_pre)
    grad_pre = gelu_back(grad_hidden)[0].astype(jnp.bfloat16)
    grad_up = jnp.dot(normed_mlp.T, grad_pre, preferred_element_type=jnp.float32)
    mlp_blocks = scatter_grads(
        (grad_up, grad_down), (up_layout, down_layout), (up_weight.shape, down_weight.shape)
    )
    grad_up, grad_down = finish_grads(*mlp_blocks)
    _, norm_back = jax.vjp(normalize, after_space, norm_gains[2])
    back_rows, gain_mlp = norm_back(
        sum_grads(jnp.dot(grad_pre, up_full.T, preferred_element_type=jnp.float32))
    )
    grad_after = grad_after + back_rows
    _, norm_back = jax.vjp(normalize, after_time, norm_gains[1])
    space_rows = spread_grads(grad_after.astype(jnp.bfloat16))
    grad_qkv_space, grad_proj_space, grad_normed = attend_backward(
        normed_space,
        space_qkv,
        space_proj,
        grouped_space,
        summary_space,
        merged_space,
        space_rows,
        False,
    )
    space_blocks = scatter_grads(
        (grad_qkv_space, grad_proj_space),
        (qkv_layout, proj_layout),
        (qkv_space.shape, proj_space.shape),
    )
    grad_qkv_space, grad_proj_space = finish_grads(*space_blocks)
    back_rows, gain_space = norm_back(sum_grads(grad_normed))
    grad_after = grad_after + back_rows
    time_rows = spread_grads(grad_after.astype(jnp.bfloat16))
    grad_qkv_time, grad_proj_time, grad_normed = attend_backward(
        normed_time, time_qkv, time_proj, grouped_time, summary_time, merged_time, time_rows, True
    )
    grad_qkv_time, grad_proj_time = finish_grads(
        *scatter_grads(
            (grad_qkv_time, grad_proj_time),
            (qkv_layout, proj_layout),
            (qkv_time.shape, proj_time.shape),
        )
    )
    _, norm_back = jax.vjp(normalize, inputs, norm_gains[0])
    back_rows, gain_time = norm_back(sum_grads(grad_normed))
    grad_tokens = grad_after + back_rows
    grad_gains = lax.psum(jnp.stack([gain_time, gain_space, gain_mlp]), ("dp", "ty", "core"))
    return (
        output,
        grad_tokens,
        grad_gains,
        grad_qkv_time,
        grad_proj_time,
        grad_qkv_space,
        grad_proj_space,
        grad_up,
        grad_down,
    )


def solution(mesh):
    def run(*args):
        rows_here = args[0].shape[0] // mesh.size
        cores = FRAMES * PATCH // rows_here
        tensor = mesh.shape["tensor"]
        assert tensor % cores == 0
        devices = mesh.devices.reshape(mesh.shape["dp"], tensor // cores, cores)
        chips = Mesh(devices, ("dp", "ty", "core"))
        rows = P(("dp", "ty", "core"), None)
        qkv = P("dp", None, ("ty", "core"))
        proj = P(("ty", "core"), "dp")
        up = P("dp", ("ty", "core"))
        down = P(("ty", "core"), "dp")
        mapped = jax.shard_map(
            per_device,
            mesh=chips,
            in_specs=(rows, rows, P(), qkv, proj, qkv, proj, up, down),
            out_specs=(rows, rows, P(), qkv, proj, qkv, proj, up, down),
            check_vma=False,
        )
        return mapped(*args)

    return run
```

```python
from functools import partial
import math

import jax
import jax.numpy as jnp
from jax import lax
from jax.sharding import Mesh, PartitionSpec as P


HD = 64
FRAMES = 8
PATCH = 196


epsilon = 1e-06


def normalize(values, gain_row):
    center = values - jnp.mean(values, axis=-1, keepdims=True)
    spread = jnp.mean(center * center, axis=-1, keepdims=True)
    return center * lax.rsqrt(spread + epsilon) * gain_row


def to_groups(values, temporal):
    trailing = values.shape[1:]
    if temporal:
        clip_count = values.shape[0] // (FRAMES * PATCH)
        shaped = values.reshape((clip_count, FRAMES, PATCH) + trailing)
        shaped = jnp.swapaxes(shaped, 1, 2)
        return shaped.reshape((clip_count * PATCH, FRAMES) + trailing)
    return values.reshape((-1, PATCH) + trailing)


def from_groups(values, temporal):
    trailing = values.shape[2:]
    if temporal:
        clip_count = values.shape[0] // PATCH
        values = jnp.swapaxes(values.reshape((clip_count, PATCH, FRAMES) + trailing), 1, 2)
    return values.reshape((-1,) + trailing)


def attend_forward(normed, w_qkv, temporal):
    factor = 1.0 / math.sqrt(HD)
    width_here = w_qkv.shape[2]
    mixed_qkv = jnp.dot(
        normed, w_qkv.reshape(w_qkv.shape[0], 3 * width_here), preferred_element_type=jnp.float32
    )
    mixed_qkv = mixed_qkv.astype(jnp.bfloat16).reshape(normed.shape[0], 3, width_here // HD, HD)
    grouped = to_groups(mixed_qkv, temporal)
    scores = (
        jnp.einsum(
            "blhe,bmhe->bhlm",
            grouped[:, :, 0],
            grouped[:, :, 1],
            preferred_element_type=jnp.float32,
        )
        * factor
    )
    row_top = jnp.max(scores, axis=-1, keepdims=True)
    shifted = jnp.exp(scores - row_top)
    row_total = jnp.sum(shifted, axis=-1, keepdims=True)
    attn_probs = (shifted / row_total).astype(jnp.bfloat16)
    attended = jnp.einsum(
        "bhlm,bmhe->blhe", attn_probs, grouped[:, :, 2], preferred_element_type=jnp.float32
    )
    merged = from_groups(attended.astype(jnp.bfloat16), temporal).reshape(
        normed.shape[0], width_here
    )
    return (grouped, row_top + jnp.log(row_total), merged)


def attend_backward(normed, w_qkv, w_proj, grouped, summary, merged, grad_rows, temporal):
    factor = 1.0 / math.sqrt(HD)
    width_here = merged.shape[1]
    grad_proj = jnp.dot(merged.T, grad_rows, preferred_element_type=jnp.float32)
    grad_merged = jnp.dot(grad_rows, w_proj.T, preferred_element_type=jnp.float32).astype(
        jnp.bfloat16
    )
    grad_attended = to_groups(grad_merged.reshape(normed.shape[0], width_here // HD, HD), temporal)
    query_rows = grouped[:, :, 0]
    key_rows = grouped[:, :, 1]
    value_rows = grouped[:, :, 2]
    scores = (
        jnp.einsum("blhe,bmhe->bhlm", query_rows, key_rows, preferred_element_type=jnp.float32)
        * factor
    )
    attn_probs = jnp.exp(scores - summary)
    grad_value = jnp.einsum(
        "bhlm,blhe->bmhe",
        attn_probs.astype(jnp.bfloat16),
        grad_attended,
        preferred_element_type=jnp.float32,
    )
    grad_probs = jnp.einsum(
        "blhe,bmhe->bhlm", grad_attended, value_rows, preferred_element_type=jnp.float32
    )
    grad_scores = attn_probs * (
        grad_probs - jnp.sum(grad_probs * attn_probs, axis=-1, keepdims=True)
    )
    grad_scores = grad_scores.astype(jnp.bfloat16)
    grad_query = (
        jnp.einsum("bhlm,bmhe->blhe", grad_scores, key_rows, preferred_element_type=jnp.float32)
        * factor
    )
    grad_key = (
        jnp.einsum("bhlm,blhe->bmhe", grad_scores, query_rows, preferred_element_type=jnp.float32)
        * factor
    )
    stacked = jnp.stack([grad_query, grad_key, grad_value], axis=2).astype(jnp.bfloat16)
    grad_mixed = from_groups(stacked, temporal).reshape(normed.shape[0], 3 * width_here)
    grad_qkv = jnp.dot(normed.T, grad_mixed, preferred_element_type=jnp.float32).reshape(
        normed.shape[1], 3, width_here
    )
    grad_normed = jnp.dot(
        grad_mixed,
        w_qkv.reshape(w_qkv.shape[0], 3 * width_here).T,
        preferred_element_type=jnp.float32,
    )
    return (grad_qkv, grad_proj, grad_normed)


WEIGHT_AXES = ("dp", "ty")


def gather_weights(shards, layouts):
    lane = 768
    flat = [w.astype(jnp.bfloat16).reshape(-1, lane) for w in shards]
    sizes = [f.shape[0] for f in flat]
    ny = lax.axis_size("ty")
    nd = lax.axis_size("dp")
    whole = lax.all_gather(jnp.concatenate(flat, axis=0), WEIGHT_AXES, axis=0, tiled=False)
    out = []
    offset = 0
    for w, size, (dp_dim, ty_dim) in zip(shards, sizes, layouts):
        part = whole[:, offset : offset + size].reshape((nd, ny) + w.shape)
        offset += size
        order = []
        for dim in range(w.ndim):
            if dim == dp_dim:
                order.append(0)
            if dim == ty_dim:
                order.append(1)
            order.append(dim + 2)
        shape = list(w.shape)
        shape[dp_dim] *= nd
        shape[ty_dim] *= ny
        out.append(jnp.transpose(part, order).reshape(shape))
    return out


def scatter_grads(grads, layouts, shard_shapes):
    ny = lax.axis_size("ty")
    nd = lax.axis_size("dp")
    assert ny == 2
    flat = []
    for g, (dp_dim, ty_dim), shard in zip(grads, layouts, shard_shapes):
        split = []
        for dim in range(g.ndim):
            if dim == dp_dim:
                split.extend([nd, shard[dim]])
            elif dim == ty_dim:
                split.extend([ny, shard[dim]])
            else:
                split.append(shard[dim])
        parts = g.reshape(split)
        pos = 0
        ty_pos = dp_pos = None
        rest = []
        for dim in range(g.ndim):
            if dim == dp_dim:
                dp_pos = pos
                rest.append(pos + 1)
                pos += 2
            elif dim == ty_dim:
                ty_pos = pos
                rest.append(pos + 1)
                pos += 2
            else:
                rest.append(pos)
                pos += 1
        flat.append(
            jnp.transpose(parts, [dp_pos, ty_pos] + rest)
            .reshape(nd, ny, -1, 768)
            .astype(jnp.bfloat16)
        )
    sizes = [f.shape[2] for f in flat]
    stacked = jnp.concatenate(flat, axis=2)
    rows = stacked.shape[2]
    blocks = lax.psum_scatter(
        stacked.reshape(-1, 768), "dp", scatter_dimension=0, tiled=True
    ).reshape(ny, rows, 768)
    return blocks, sizes, shard_shapes


def finish_grads(blocks, sizes, shard_shapes):
    here = lax.axis_index("ty")
    own = lax.dynamic_index_in_dim(blocks, here, axis=0, keepdims=False)
    other = lax.dynamic_index_in_dim(blocks, 1 - here, axis=0, keepdims=False)
    summed = own.astype(jnp.float32) + swap_ty(other).astype(jnp.float32)
    out = []
    offset = 0
    for size, shard in zip(sizes, shard_shapes):
        out.append(summed[offset : offset + size].reshape(shard))
        offset += size
    return out


def swap_ty(values):
    return lax.ppermute(values, "ty", perm=[(0, 1), (1, 0)])


def per_device(
    tokens,
    cotangent,
    norm_gains,
    qkv_time,
    proj_time,
    qkv_space,
    proj_space,
    up_weight,
    down_weight,
):
    qkv_layout = (0, 2)
    proj_layout = (1, 0)
    up_layout = (0, 1)
    down_layout = (1, 0)
    time_qkv, time_proj = gather_weights((qkv_time, proj_time), (qkv_layout, proj_layout))
    space_qkv, space_proj = gather_weights((qkv_space, proj_space), (qkv_layout, proj_layout))
    up_full, down_full = gather_weights((up_weight, down_weight), (up_layout, down_layout))

    def swap(values):
        return lax.ppermute(values, "core", perm=[(0, 1), (1, 0)])

    def spread_rows(values):
        return jnp.concatenate([values, swap(values)], axis=0)

    def sum_rows(values):
        half = values.shape[0] // 2
        return values[:half] + swap(values[half:].astype(jnp.bfloat16)).astype(jnp.float32)

    spread_grads = spread_rows
    sum_grads = sum_rows

    inputs = tokens.astype(jnp.float32)
    normed_time = spread_rows(normalize(inputs, norm_gains[0]).astype(jnp.bfloat16))
    grouped_time, summary_time, merged_time = attend_forward(normed_time, time_qkv, True)
    after_time = inputs + sum_rows(
        jnp.dot(merged_time, time_proj, preferred_element_type=jnp.float32)
    )
    normed_space = spread_rows(normalize(after_time, norm_gains[1]).astype(jnp.bfloat16))
    grouped_space, summary_space, merged_space = attend_forward(normed_space, space_qkv, False)
    after_space = after_time + sum_rows(
        jnp.dot(merged_space, space_proj, preferred_element_type=jnp.float32)
    )
    normed_mlp = spread_rows(normalize(after_space, norm_gains[2]).astype(jnp.bfloat16))
    hidden_pre = jnp.dot(normed_mlp, up_full, preferred_element_type=jnp.float32)
    hidden = jax.nn.gelu(hidden_pre, approximate=False).astype(jnp.bfloat16)
    output = (
        after_space + sum_rows(jnp.dot(hidden, down_full, preferred_element_type=jnp.float32))
    ).astype(jnp.bfloat16)

    grad_after = cotangent.astype(jnp.float32)
    down_rows = spread_grads(grad_after.astype(jnp.bfloat16))
    grad_down = jnp.dot(hidden.T, down_rows, preferred_element_type=jnp.float32)
    grad_hidden = jnp.dot(down_rows, down_full.T, preferred_element_type=jnp.float32)
    _, gelu_back = jax.vjp(partial(jax.nn.gelu, approximate=False), hidden_pre)
    grad_pre = gelu_back(grad_hidden)[0].astype(jnp.bfloat16)
    grad_up = jnp.dot(normed_mlp.T, grad_pre, preferred_element_type=jnp.float32)
    mlp_blocks = scatter_grads(
        (grad_up, grad_down), (up_layout, down_layout), (up_weight.shape, down_weight.shape)
    )
    grad_up, grad_down = finish_grads(*mlp_blocks)
    _, norm_back = jax.vjp(normalize, after_space, norm_gains[2])
    back_rows, gain_mlp = norm_back(
        sum_grads(jnp.dot(grad_pre, up_full.T, preferred_element_type=jnp.float32))
    )
    grad_after = grad_after + back_rows
    _, norm_back = jax.vjp(normalize, after_time, norm_gains[1])
    space_rows = spread_grads(grad_after.astype(jnp.bfloat16))
    grad_qkv_space, grad_proj_space, grad_normed = attend_backward(
        normed_space,
        space_qkv,
        space_proj,
        grouped_space,
        summary_space,
        merged_space,
        space_rows,
        False,
    )
    space_blocks = scatter_grads(
        (grad_qkv_space, grad_proj_space),
        (qkv_layout, proj_layout),
        (qkv_space.shape, proj_space.shape),
    )
    grad_qkv_space, grad_proj_space = finish_grads(*space_blocks)
    back_rows, gain_space = norm_back(sum_grads(grad_normed))
    grad_after = grad_after + back_rows
    time_rows = spread_grads(grad_after.astype(jnp.bfloat16))
    grad_qkv_time, grad_proj_time, grad_normed = attend_backward(
        normed_time, time_qkv, time_proj, grouped_time, summary_time, merged_time, time_rows, True
    )
    grad_qkv_time, grad_proj_time = finish_grads(
        *scatter_grads(
            (grad_qkv_time, grad_proj_time),
            (qkv_layout, proj_layout),
            (qkv_time.shape, proj_time.shape),
        )
    )
    _, norm_back = jax.vjp(normalize, inputs, norm_gains[0])
    back_rows, gain_time = norm_back(sum_grads(grad_normed))
    grad_tokens = grad_after + back_rows
    grad_gains = lax.psum(jnp.stack([gain_time, gain_space, gain_mlp]), ("dp", "ty", "core"))
    return (
        output,
        grad_tokens,
        grad_gains,
        grad_qkv_time,
        grad_proj_time,
        grad_qkv_space,
        grad_proj_space,
        grad_up,
        grad_down,
    )


def solution(mesh):
    def run(*args):
        rows_here = args[0].shape[0] // mesh.size
        cores = FRAMES * PATCH // rows_here
        tensor = mesh.shape["tensor"]
        assert tensor % cores == 0
        devices = mesh.devices.reshape(mesh.shape["dp"], tensor // cores, cores)
        chips = Mesh(devices, ("dp", "ty", "core"))
        rows = P(("dp", "ty", "core"), None)
        qkv = P("dp", None, ("ty", "core"))
        proj = P(("ty", "core"), "dp")
        up = P("dp", ("ty", "core"))
        down = P(("ty", "core"), "dp")
        mapped = jax.shard_map(
            per_device,
            mesh=chips,
            in_specs=(rows, rows, P(), qkv, proj, qkv, proj, up, down),
            out_specs=(rows, rows, P(), qkv, proj, qkv, proj, up, down),
            check_vma=False,
        )
        return mapped(*args)

    return run
```

```python
from functools import partial
import math

import jax
import jax.numpy as jnp
from jax import lax
from jax.sharding import Mesh, PartitionSpec as P


HD = 64
FRAMES = 8
PATCH = 196


epsilon = 1e-06


def normalize(values, gain_row):
    center = values - jnp.mean(values, axis=-1, keepdims=True)
    spread = jnp.mean(center * center, axis=-1, keepdims=True)
    return center * lax.rsqrt(spread + epsilon) * gain_row


def to_groups(values, temporal):
    trailing = values.shape[1:]
    if temporal:
        clip_count = values.shape[0] // (FRAMES * PATCH)
        shaped = values.reshape((clip_count, FRAMES, PATCH) + trailing)
        shaped = jnp.swapaxes(shaped, 1, 2)
        return shaped.reshape((clip_count * PATCH, FRAMES) + trailing)
    return values.reshape((-1, PATCH) + trailing)


def from_groups(values, temporal):
    trailing = values.shape[2:]
    if temporal:
        clip_count = values.shape[0] // PATCH
        values = jnp.swapaxes(values.reshape((clip_count, PATCH, FRAMES) + trailing), 1, 2)
    return values.reshape((-1,) + trailing)


def attend_forward(normed, w_qkv, temporal):
    factor = 1.0 / math.sqrt(HD)
    width_here = w_qkv.shape[2]
    mixed_qkv = jnp.dot(
        normed, w_qkv.reshape(w_qkv.shape[0], 3 * width_here), preferred_element_type=jnp.float32
    )
    mixed_qkv = mixed_qkv.astype(jnp.bfloat16).reshape(normed.shape[0], 3, width_here // HD, HD)
    grouped = to_groups(mixed_qkv, temporal)
    scores = (
        jnp.einsum(
            "blhe,bmhe->bhlm",
            grouped[:, :, 0],
            grouped[:, :, 1],
            preferred_element_type=jnp.float32,
        )
        * factor
    )
    row_top = jnp.max(scores, axis=-1, keepdims=True)
    shifted = jnp.exp(scores - row_top)
    row_total = jnp.sum(shifted, axis=-1, keepdims=True)
    attn_probs = (shifted / row_total).astype(jnp.bfloat16)
    attended = jnp.einsum(
        "bhlm,bmhe->blhe", attn_probs, grouped[:, :, 2], preferred_element_type=jnp.float32
    )
    merged = from_groups(attended.astype(jnp.bfloat16), temporal).reshape(
        normed.shape[0], width_here
    )
    return (grouped, row_top + jnp.log(row_total), merged)


def attend_backward(normed, w_qkv, w_proj, grouped, summary, merged, grad_rows, temporal):
    factor = 1.0 / math.sqrt(HD)
    width_here = merged.shape[1]
    grad_proj = jnp.dot(merged.T, grad_rows, preferred_element_type=jnp.float32)
    grad_merged = jnp.dot(grad_rows, w_proj.T, preferred_element_type=jnp.float32).astype(
        jnp.bfloat16
    )
    grad_attended = to_groups(grad_merged.reshape(normed.shape[0], width_here // HD, HD), temporal)
    query_rows = grouped[:, :, 0]
    key_rows = grouped[:, :, 1]
    value_rows = grouped[:, :, 2]
    scores = (
        jnp.einsum("blhe,bmhe->bhlm", query_rows, key_rows, preferred_element_type=jnp.float32)
        * factor
    )
    attn_probs = jnp.exp(scores - summary)
    grad_value = jnp.einsum(
        "bhlm,blhe->bmhe",
        attn_probs.astype(jnp.bfloat16),
        grad_attended,
        preferred_element_type=jnp.float32,
    )
    grad_probs = jnp.einsum(
        "blhe,bmhe->bhlm", grad_attended, value_rows, preferred_element_type=jnp.float32
    )
    grad_scores = attn_probs * (
        grad_probs - jnp.sum(grad_probs * attn_probs, axis=-1, keepdims=True)
    )
    grad_scores = grad_scores.astype(jnp.bfloat16)
    grad_query = (
        jnp.einsum("bhlm,bmhe->blhe", grad_scores, key_rows, preferred_element_type=jnp.float32)
        * factor
    )
    grad_key = (
        jnp.einsum("bhlm,blhe->bmhe", grad_scores, query_rows, preferred_element_type=jnp.float32)
        * factor
    )
    stacked = jnp.stack([grad_query, grad_key, grad_value], axis=2).astype(jnp.bfloat16)
    grad_mixed = from_groups(stacked, temporal).reshape(normed.shape[0], 3 * width_here)
    grad_qkv = jnp.dot(normed.T, grad_mixed, preferred_element_type=jnp.float32).reshape(
        normed.shape[1], 3, width_here
    )
    grad_normed = jnp.dot(
        grad_mixed,
        w_qkv.reshape(w_qkv.shape[0], 3 * width_here).T,
        preferred_element_type=jnp.float32,
    )
    return (grad_qkv, grad_proj, grad_normed)


def gather_attention(qkv_shard, proj_shard):
    rows, parts, width = qkv_shard.shape
    mine = jnp.concatenate(
        [qkv_shard.astype(jnp.bfloat16).reshape(rows, parts * width), proj_shard.astype(jnp.bfloat16).T],
        axis=1,
    )
    other = swap_ty(mine)
    split = parts * width
    qkv_local = jnp.stack(
        [mine[:, :split].reshape(rows, parts, width), other[:, :split].reshape(rows, parts, width)],
        axis=2,
    ).reshape(rows, 2 * split)
    proj_local = jnp.concatenate([mine[:, split:], other[:, split:]], axis=1)
    full = lax.all_gather(
        jnp.concatenate([qkv_local, proj_local], axis=1), "dp", axis=0, tiled=True
    )
    w_qkv = full[:, : 2 * split].reshape(full.shape[0], parts, 2 * width)
    w_proj = full[:, 2 * split :].T
    return w_qkv, w_proj


def gather_mlp(up_shard, down_shard):
    width = up_shard.shape[1]
    mine = jnp.concatenate(
        [up_shard.astype(jnp.bfloat16), down_shard.astype(jnp.bfloat16).T], axis=1
    )
    other = swap_ty(mine)
    local = jnp.concatenate(
        [mine[:, :width], other[:, :width], mine[:, width:], other[:, width:]], axis=1
    )
    full = lax.all_gather(local, "dp", axis=0, tiled=True)
    return full[:, : 2 * width], full[:, 2 * width :].T


def scatter_grads(grads, layouts, shard_shapes):
    ny = lax.axis_size("ty")
    nd = lax.axis_size("dp")
    assert ny == 2
    flat = []
    for g, (dp_dim, ty_dim), shard in zip(grads, layouts, shard_shapes):
        split = []
        for dim in range(g.ndim):
            if dim == dp_dim:
                split.extend([nd, shard[dim]])
            elif dim == ty_dim:
                split.extend([ny, shard[dim]])
            else:
                split.append(shard[dim])
        parts = g.reshape(split)
        pos = 0
        ty_pos = dp_pos = None
        rest = []
        for dim in range(g.ndim):
            if dim == dp_dim:
                dp_pos = pos
                rest.append(pos + 1)
                pos += 2
            elif dim == ty_dim:
                ty_pos = pos
                rest.append(pos + 1)
                pos += 2
            else:
                rest.append(pos)
                pos += 1
        flat.append(
            jnp.transpose(parts, [dp_pos, ty_pos] + rest)
            .reshape(nd, ny, -1, 768)
            .astype(jnp.bfloat16)
        )
    sizes = [f.shape[2] for f in flat]
    stacked = jnp.concatenate(flat, axis=2)
    rows = stacked.shape[2]
    blocks = lax.psum_scatter(
        stacked.reshape(-1, 768), "dp", scatter_dimension=0, tiled=True
    ).reshape(ny, rows, 768)
    return blocks, sizes, shard_shapes


def finish_grads(blocks, sizes, shard_shapes):
    summed = blocks[0].astype(jnp.float32) + swap_ty(blocks[1]).astype(jnp.float32)
    out = []
    offset = 0
    for size, shard in zip(sizes, shard_shapes):
        out.append(summed[offset : offset + size].reshape(shard))
        offset += size
    return out


def swap_ty(values):
    return lax.ppermute(values, "ty", perm=[(0, 1), (1, 0)])


def per_device(
    tokens,
    cotangent,
    norm_gains,
    qkv_time,
    proj_time,
    qkv_space,
    proj_space,
    up_weight,
    down_weight,
):
    qkv_layout = (0, 2)
    proj_layout = (1, 0)
    up_layout = (0, 1)
    down_layout = (1, 0)
    time_qkv, time_proj = gather_attention(qkv_time, proj_time)
    space_qkv, space_proj = gather_attention(qkv_space, proj_space)
    up_full, down_full = gather_mlp(up_weight, down_weight)

    def swap(values):
        return lax.ppermute(values, "core", perm=[(0, 1), (1, 0)])

    def spread_rows(values):
        return jnp.concatenate([values, swap(values)], axis=0)

    def sum_rows(values):
        half = values.shape[0] // 2
        return values[:half] + swap(values[half:].astype(jnp.bfloat16)).astype(jnp.float32)

    spread_grads = spread_rows
    sum_grads = sum_rows

    inputs = tokens.astype(jnp.float32)
    normed_time = spread_rows(normalize(inputs, norm_gains[0]).astype(jnp.bfloat16))
    grouped_time, summary_time, merged_time = attend_forward(normed_time, time_qkv, True)
    after_time = inputs + sum_rows(
        jnp.dot(merged_time, time_proj, preferred_element_type=jnp.float32)
    )
    normed_space = spread_rows(normalize(after_time, norm_gains[1]).astype(jnp.bfloat16))
    grouped_space, summary_space, merged_space = attend_forward(normed_space, space_qkv, False)
    after_space = after_time + sum_rows(
        jnp.dot(merged_space, space_proj, preferred_element_type=jnp.float32)
    )
    normed_mlp = spread_rows(normalize(after_space, norm_gains[2]).astype(jnp.bfloat16))
    hidden_pre = jnp.dot(normed_mlp, up_full, preferred_element_type=jnp.float32)
    hidden = jax.nn.gelu(hidden_pre, approximate=False).astype(jnp.bfloat16)
    output = (
        after_space + sum_rows(jnp.dot(hidden, down_full, preferred_element_type=jnp.float32))
    ).astype(jnp.bfloat16)

    grad_after = cotangent.astype(jnp.float32)
    down_rows = spread_grads(grad_after.astype(jnp.bfloat16))
    grad_down = jnp.dot(hidden.T, down_rows, preferred_element_type=jnp.float32)
    grad_hidden = jnp.dot(down_rows, down_full.T, preferred_element_type=jnp.float32)
    _, gelu_back = jax.vjp(partial(jax.nn.gelu, approximate=False), hidden_pre)
    grad_pre = gelu_back(grad_hidden)[0].astype(jnp.bfloat16)
    grad_up = jnp.dot(normed_mlp.T, grad_pre, preferred_element_type=jnp.float32)
    mlp_blocks = scatter_grads(
        (grad_up, grad_down), (up_layout, down_layout), (up_weight.shape, down_weight.shape)
    )
    grad_up, grad_down = finish_grads(*mlp_blocks)
    _, norm_back = jax.vjp(normalize, after_space, norm_gains[2])
    back_rows, gain_mlp = norm_back(
        sum_grads(jnp.dot(grad_pre, up_full.T, preferred_element_type=jnp.float32))
    )
    grad_after = grad_after + back_rows
    _, norm_back = jax.vjp(normalize, after_time, norm_gains[1])
    space_rows = spread_grads(grad_after.astype(jnp.bfloat16))
    grad_qkv_space, grad_proj_space, grad_normed = attend_backward(
        normed_space,
        space_qkv,
        space_proj,
        grouped_space,
        summary_space,
        merged_space,
        space_rows,
        False,
    )
    space_blocks = scatter_grads(
        (grad_qkv_space, grad_proj_space),
        (qkv_layout, proj_layout),
        (qkv_space.shape, proj_space.shape),
    )
    grad_qkv_space, grad_proj_space = finish_grads(*space_blocks)
    back_rows, gain_space = norm_back(sum_grads(grad_normed))
    grad_after = grad_after + back_rows
    time_rows = spread_grads(grad_after.astype(jnp.bfloat16))
    grad_qkv_time, grad_proj_time, grad_normed = attend_backward(
        normed_time, time_qkv, time_proj, grouped_time, summary_time, merged_time, time_rows, True
    )
    grad_qkv_time, grad_proj_time = finish_grads(
        *scatter_grads(
            (grad_qkv_time, grad_proj_time),
            (qkv_layout, proj_layout),
            (qkv_time.shape, proj_time.shape),
        )
    )
    _, norm_back = jax.vjp(normalize, inputs, norm_gains[0])
    back_rows, gain_time = norm_back(sum_grads(grad_normed))
    grad_tokens = grad_after + back_rows
    grad_gains = lax.psum(jnp.stack([gain_time, gain_space, gain_mlp]), ("dp", "ty", "core"))
    return (
        output,
        grad_tokens,
        grad_gains,
        grad_qkv_time,
        grad_proj_time,
        grad_qkv_space,
        grad_proj_space,
        grad_up,
        grad_down,
    )


def solution(mesh):
    def run(*args):
        rows_here = args[0].shape[0] // mesh.size
        cores = FRAMES * PATCH // rows_here
        tensor = mesh.shape["tensor"]
        assert tensor % cores == 0
        devices = mesh.devices.reshape(mesh.shape["dp"], tensor // cores, cores)
        chips = Mesh(devices, ("dp", "ty", "core"))
        rows = P(("dp", "ty", "core"), None)
        qkv = P("dp", None, ("ty", "core"))
        proj = P(("ty", "core"), "dp")
        up = P("dp", ("ty", "core"))
        down = P(("ty", "core"), "dp")
        mapped = jax.shard_map(
            per_device,
            mesh=chips,
            in_specs=(rows, rows, P(), qkv, proj, qkv, proj, up, down),
            out_specs=(rows, rows, P(), qkv, proj, qkv, proj, up, down),
            check_vma=False,
        )
        return mapped(*args)

    return run
```

```python
from functools import partial
import math

import jax
import jax.numpy as jnp
from jax import lax
from jax.sharding import Mesh, PartitionSpec as P


HD = 64
FRAMES = 8
PATCH = 196


epsilon = 1e-06


def normalize(values, gain_row):
    center = values - jnp.mean(values, axis=-1, keepdims=True)
    spread = jnp.mean(center * center, axis=-1, keepdims=True)
    return center * lax.rsqrt(spread + epsilon) * gain_row


def to_groups(values, temporal):
    trailing = values.shape[1:]
    if temporal:
        clip_count = values.shape[0] // (FRAMES * PATCH)
        shaped = values.reshape((clip_count, FRAMES, PATCH) + trailing)
        shaped = jnp.swapaxes(shaped, 1, 2)
        return shaped.reshape((clip_count * PATCH, FRAMES) + trailing)
    return values.reshape((-1, PATCH) + trailing)


def from_groups(values, temporal):
    trailing = values.shape[2:]
    if temporal:
        clip_count = values.shape[0] // PATCH
        values = jnp.swapaxes(values.reshape((clip_count, PATCH, FRAMES) + trailing), 1, 2)
    return values.reshape((-1,) + trailing)


def attend_forward(normed, w_qkv, temporal):
    factor = 1.0 / math.sqrt(HD)
    width_here = w_qkv.shape[2]
    mixed_qkv = jnp.dot(
        normed, w_qkv.reshape(w_qkv.shape[0], 3 * width_here), preferred_element_type=jnp.float32
    )
    mixed_qkv = mixed_qkv.astype(jnp.bfloat16).reshape(normed.shape[0], 3, width_here // HD, HD)
    grouped = to_groups(mixed_qkv, temporal)
    scores = (
        jnp.einsum(
            "blhe,bmhe->bhlm",
            grouped[:, :, 0],
            grouped[:, :, 1],
            preferred_element_type=jnp.float32,
        )
        * factor
    )
    row_top = jnp.max(scores, axis=-1, keepdims=True)
    shifted = jnp.exp(scores - row_top)
    row_total = jnp.sum(shifted, axis=-1, keepdims=True)
    attn_probs = (shifted / row_total).astype(jnp.bfloat16)
    attended = jnp.einsum(
        "bhlm,bmhe->blhe", attn_probs, grouped[:, :, 2], preferred_element_type=jnp.float32
    )
    merged = from_groups(attended.astype(jnp.bfloat16), temporal).reshape(
        normed.shape[0], width_here
    )
    return (grouped, row_top + jnp.log(row_total), merged)


def attend_backward(normed, w_qkv, w_proj, grouped, summary, merged, grad_rows, temporal):
    factor = 1.0 / math.sqrt(HD)
    width_here = merged.shape[1]
    grad_proj = jnp.dot(grad_rows.T, merged, preferred_element_type=jnp.float32)
    grad_merged = jnp.dot(grad_rows, w_proj.T, preferred_element_type=jnp.float32).astype(
        jnp.bfloat16
    )
    grad_attended = to_groups(grad_merged.reshape(normed.shape[0], width_here // HD, HD), temporal)
    query_rows = grouped[:, :, 0]
    key_rows = grouped[:, :, 1]
    value_rows = grouped[:, :, 2]
    scores = (
        jnp.einsum("blhe,bmhe->bhlm", query_rows, key_rows, preferred_element_type=jnp.float32)
        * factor
    )
    attn_probs = jnp.exp(scores - summary)
    grad_value = jnp.einsum(
        "bhlm,blhe->bmhe",
        attn_probs.astype(jnp.bfloat16),
        grad_attended,
        preferred_element_type=jnp.float32,
    )
    grad_probs = jnp.einsum(
        "blhe,bmhe->bhlm", grad_attended, value_rows, preferred_element_type=jnp.float32
    )
    grad_scores = attn_probs * (
        grad_probs - jnp.sum(grad_probs * attn_probs, axis=-1, keepdims=True)
    )
    grad_scores = grad_scores.astype(jnp.bfloat16)
    grad_query = (
        jnp.einsum("bhlm,bmhe->blhe", grad_scores, key_rows, preferred_element_type=jnp.float32)
        * factor
    )
    grad_key = (
        jnp.einsum("bhlm,blhe->bmhe", grad_scores, query_rows, preferred_element_type=jnp.float32)
        * factor
    )
    stacked = jnp.stack([grad_query, grad_key, grad_value], axis=2).astype(jnp.bfloat16)
    grad_mixed = from_groups(stacked, temporal).reshape(normed.shape[0], 3 * width_here)
    grad_qkv = jnp.dot(normed.T, grad_mixed, preferred_element_type=jnp.float32).reshape(
        normed.shape[1], 3, width_here
    )
    grad_normed = jnp.dot(
        grad_mixed,
        w_qkv.reshape(w_qkv.shape[0], 3 * width_here).T,
        preferred_element_type=jnp.float32,
    )
    return (grad_qkv, grad_proj, grad_normed)


def gather_attention(qkv_shard, proj_shard):
    rows, parts, width = qkv_shard.shape
    mine = jnp.concatenate(
        [qkv_shard.astype(jnp.bfloat16).reshape(rows, parts * width), proj_shard.astype(jnp.bfloat16).T],
        axis=1,
    )
    other = swap_ty(mine)
    split = parts * width
    qkv_local = jnp.stack(
        [mine[:, :split].reshape(rows, parts, width), other[:, :split].reshape(rows, parts, width)],
        axis=2,
    ).reshape(rows, 2 * split)
    proj_local = jnp.concatenate([mine[:, split:], other[:, split:]], axis=1)
    full = lax.all_gather(
        jnp.concatenate([qkv_local, proj_local], axis=1), "dp", axis=0, tiled=True
    )
    w_qkv = full[:, : 2 * split].reshape(full.shape[0], parts, 2 * width)
    w_proj = full[:, 2 * split :].T
    return w_qkv, w_proj


def gather_mlp(up_shard, down_shard):
    width = up_shard.shape[1]
    mine = jnp.concatenate(
        [up_shard.astype(jnp.bfloat16), down_shard.astype(jnp.bfloat16).T], axis=1
    )
    other = swap_ty(mine)
    local = jnp.concatenate(
        [mine[:, :width], other[:, :width], mine[:, width:], other[:, width:]], axis=1
    )
    full = lax.all_gather(local, "dp", axis=0, tiled=True)
    return full[:, : 2 * width], full[:, 2 * width :].T


def scatter_rows(pieces):
    flat = [p.reshape(p.shape[0], -1) for p in pieces]
    return lax.psum_scatter(
        jnp.concatenate(flat, axis=1).astype(jnp.bfloat16), "dp", scatter_dimension=0, tiled=True
    )


def finish_attention(local, qkv_shape, proj_shape):
    rows, parts, width = qkv_shape
    split = parts * 2 * width
    qkv = local[:, :split].reshape(rows, parts, 2, width)
    proj = local[:, split:]
    half = proj.shape[1] // 2
    mine = jnp.concatenate([qkv[:, :, 0].reshape(rows, -1), proj[:, :half]], axis=1)
    other = jnp.concatenate([qkv[:, :, 1].reshape(rows, -1), proj[:, half:]], axis=1)
    summed = mine.astype(jnp.float32) + swap_ty(other).astype(jnp.float32)
    return summed[:, : parts * width].reshape(qkv_shape), summed[:, parts * width :].T.reshape(proj_shape)


def finish_mlp(local, up_shape, down_shape):
    width = up_shape[1]
    mine = jnp.concatenate([local[:, :width], local[:, 2 * width : 3 * width]], axis=1)
    other = jnp.concatenate([local[:, width : 2 * width], local[:, 3 * width :]], axis=1)
    summed = mine.astype(jnp.float32) + swap_ty(other).astype(jnp.float32)
    return summed[:, :width].reshape(up_shape), summed[:, width:].T.reshape(down_shape)


def swap_ty(values):
    return lax.ppermute(values, "ty", perm=[(0, 1), (1, 0)])


def per_device(
    tokens,
    cotangent,
    norm_gains,
    qkv_time,
    proj_time,
    qkv_space,
    proj_space,
    up_weight,
    down_weight,
):
    time_qkv, time_proj = gather_attention(qkv_time, proj_time)
    space_qkv, space_proj = gather_attention(qkv_space, proj_space)
    up_full, down_full = gather_mlp(up_weight, down_weight)

    def swap(values):
        return lax.ppermute(values, "core", perm=[(0, 1), (1, 0)])

    def spread_rows(values):
        return jnp.concatenate([values, swap(values)], axis=0)

    def sum_rows(values):
        half = values.shape[0] // 2
        return values[:half] + swap(values[half:].astype(jnp.bfloat16)).astype(jnp.float32)

    spread_grads = spread_rows
    sum_grads = sum_rows

    inputs = tokens.astype(jnp.float32)
    normed_time = spread_rows(normalize(inputs, norm_gains[0]).astype(jnp.bfloat16))
    grouped_time, summary_time, merged_time = attend_forward(normed_time, time_qkv, True)
    after_time = inputs + sum_rows(
        jnp.dot(merged_time, time_proj, preferred_element_type=jnp.float32)
    )
    normed_space = spread_rows(normalize(after_time, norm_gains[1]).astype(jnp.bfloat16))
    grouped_space, summary_space, merged_space = attend_forward(normed_space, space_qkv, False)
    after_space = after_time + sum_rows(
        jnp.dot(merged_space, space_proj, preferred_element_type=jnp.float32)
    )
    normed_mlp = spread_rows(normalize(after_space, norm_gains[2]).astype(jnp.bfloat16))
    hidden_pre = jnp.dot(normed_mlp, up_full, preferred_element_type=jnp.float32)
    hidden = jax.nn.gelu(hidden_pre, approximate=False).astype(jnp.bfloat16)
    output = (
        after_space + sum_rows(jnp.dot(hidden, down_full, preferred_element_type=jnp.float32))
    ).astype(jnp.bfloat16)

    grad_after = cotangent.astype(jnp.float32)
    down_rows = spread_grads(grad_after.astype(jnp.bfloat16))
    grad_down = jnp.dot(down_rows.T, hidden, preferred_element_type=jnp.float32)
    grad_hidden = jnp.dot(down_rows, down_full.T, preferred_element_type=jnp.float32)
    _, gelu_back = jax.vjp(partial(jax.nn.gelu, approximate=False), hidden_pre)
    grad_pre = gelu_back(grad_hidden)[0].astype(jnp.bfloat16)
    grad_up = jnp.dot(normed_mlp.T, grad_pre, preferred_element_type=jnp.float32)
    mlp_local = scatter_rows((grad_up, grad_down))
    grad_up, grad_down = finish_mlp(mlp_local, up_weight.shape, down_weight.shape)
    _, norm_back = jax.vjp(normalize, after_space, norm_gains[2])
    back_rows, gain_mlp = norm_back(
        sum_grads(jnp.dot(grad_pre, up_full.T, preferred_element_type=jnp.float32))
    )
    grad_after = grad_after + back_rows
    _, norm_back = jax.vjp(normalize, after_time, norm_gains[1])
    space_rows = spread_grads(grad_after.astype(jnp.bfloat16))
    grad_qkv_space, grad_proj_space, grad_normed = attend_backward(
        normed_space,
        space_qkv,
        space_proj,
        grouped_space,
        summary_space,
        merged_space,
        space_rows,
        False,
    )
    space_local = scatter_rows((grad_qkv_space, grad_proj_space))
    grad_qkv_space, grad_proj_space = finish_attention(space_local, qkv_space.shape, proj_space.shape)
    back_rows, gain_space = norm_back(sum_grads(grad_normed))
    grad_after = grad_after + back_rows
    time_rows = spread_grads(grad_after.astype(jnp.bfloat16))
    grad_qkv_time, grad_proj_time, grad_normed = attend_backward(
        normed_time, time_qkv, time_proj, grouped_time, summary_time, merged_time, time_rows, True
    )
    grad_qkv_time, grad_proj_time = finish_attention(
        scatter_rows((grad_qkv_time, grad_proj_time)), qkv_time.shape, proj_time.shape
    )
    _, norm_back = jax.vjp(normalize, inputs, norm_gains[0])
    back_rows, gain_time = norm_back(sum_grads(grad_normed))
    grad_tokens = grad_after + back_rows
    grad_gains = lax.psum(jnp.stack([gain_time, gain_space, gain_mlp]), ("dp", "ty", "core"))
    return (
        output,
        grad_tokens,
        grad_gains,
        grad_qkv_time,
        grad_proj_time,
        grad_qkv_space,
        grad_proj_space,
        grad_up,
        grad_down,
    )


def solution(mesh):
    def run(*args):
        rows_here = args[0].shape[0] // mesh.size
        cores = FRAMES * PATCH // rows_here
        tensor = mesh.shape["tensor"]
        assert tensor % cores == 0
        devices = mesh.devices.reshape(mesh.shape["dp"], tensor // cores, cores)
        chips = Mesh(devices, ("dp", "ty", "core"))
        rows = P(("dp", "ty", "core"), None)
        qkv = P("dp", None, ("ty", "core"))
        proj = P(("ty", "core"), "dp")
        up = P("dp", ("ty", "core"))
        down = P(("ty", "core"), "dp")
        mapped = jax.shard_map(
            per_device,
            mesh=chips,
            in_specs=(rows, rows, P(), qkv, proj, qkv, proj, up, down),
            out_specs=(rows, rows, P(), qkv, proj, qkv, proj, up, down),
            check_vma=False,
        )
        return mapped(*args)

    return run
```

```python
from functools import partial
import math

import jax
import jax.numpy as jnp
from jax import lax
from jax.sharding import Mesh, PartitionSpec as P


HD = 64
FRAMES = 8
PATCH = 196


epsilon = 1e-06


def normalize(values, gain_row):
    center = values - jnp.mean(values, axis=-1, keepdims=True)
    spread = jnp.mean(center * center, axis=-1, keepdims=True)
    return center * lax.rsqrt(spread + epsilon) * gain_row


def to_groups(values, temporal):
    trailing = values.shape[1:]
    if temporal:
        clip_count = values.shape[0] // (FRAMES * PATCH)
        shaped = values.reshape((clip_count, FRAMES, PATCH) + trailing)
        shaped = jnp.swapaxes(shaped, 1, 2)
        return shaped.reshape((clip_count * PATCH, FRAMES) + trailing)
    return values.reshape((-1, PATCH) + trailing)


def from_groups(values, temporal):
    trailing = values.shape[2:]
    if temporal:
        clip_count = values.shape[0] // PATCH
        values = jnp.swapaxes(values.reshape((clip_count, PATCH, FRAMES) + trailing), 1, 2)
    return values.reshape((-1,) + trailing)


def attend_forward(normed, w_qkv, temporal):
    factor = 1.0 / math.sqrt(HD)
    width_here = w_qkv.shape[2]
    mixed_qkv = jnp.dot(
        normed, w_qkv.reshape(w_qkv.shape[0], 3 * width_here), preferred_element_type=jnp.float32
    )
    mixed_qkv = mixed_qkv.astype(jnp.bfloat16).reshape(normed.shape[0], 3, width_here // HD, HD)
    grouped = to_groups(mixed_qkv, temporal)
    scores = (
        jnp.einsum(
            "blhe,bmhe->bhlm",
            grouped[:, :, 0],
            grouped[:, :, 1],
            preferred_element_type=jnp.float32,
        )
        * factor
    )
    row_top = jnp.max(scores, axis=-1, keepdims=True)
    shifted = jnp.exp(scores - row_top)
    row_total = jnp.sum(shifted, axis=-1, keepdims=True)
    attn_probs = (shifted / row_total).astype(jnp.bfloat16)
    attended = jnp.einsum(
        "bhlm,bmhe->blhe", attn_probs, grouped[:, :, 2], preferred_element_type=jnp.float32
    )
    merged = from_groups(attended.astype(jnp.bfloat16), temporal).reshape(
        normed.shape[0], width_here
    )
    return (grouped, row_top + jnp.log(row_total), merged)


def attend_backward(normed, w_qkv, w_proj, grouped, summary, merged, grad_rows, temporal):
    factor = 1.0 / math.sqrt(HD)
    width_here = merged.shape[1]
    grad_proj = jnp.dot(grad_rows.T, merged, preferred_element_type=jnp.float32)
    grad_merged = jnp.dot(grad_rows, w_proj.T, preferred_element_type=jnp.float32).astype(
        jnp.bfloat16
    )
    grad_attended = to_groups(grad_merged.reshape(normed.shape[0], width_here // HD, HD), temporal)
    query_rows = grouped[:, :, 0]
    key_rows = grouped[:, :, 1]
    value_rows = grouped[:, :, 2]
    scores = (
        jnp.einsum("blhe,bmhe->bhlm", query_rows, key_rows, preferred_element_type=jnp.float32)
        * factor
    )
    attn_probs = jnp.exp(scores - summary)
    grad_value = jnp.einsum(
        "bhlm,blhe->bmhe",
        attn_probs.astype(jnp.bfloat16),
        grad_attended,
        preferred_element_type=jnp.float32,
    )
    grad_probs = jnp.einsum(
        "blhe,bmhe->bhlm", grad_attended, value_rows, preferred_element_type=jnp.float32
    )
    grad_scores = attn_probs * (
        grad_probs - jnp.sum(grad_probs * attn_probs, axis=-1, keepdims=True)
    )
    grad_scores = grad_scores.astype(jnp.bfloat16)
    grad_query = (
        jnp.einsum("bhlm,bmhe->blhe", grad_scores, key_rows, preferred_element_type=jnp.float32)
        * factor
    )
    grad_key = (
        jnp.einsum("bhlm,blhe->bmhe", grad_scores, query_rows, preferred_element_type=jnp.float32)
        * factor
    )
    stacked = jnp.stack([grad_query, grad_key, grad_value], axis=2).astype(jnp.bfloat16)
    grad_mixed = from_groups(stacked, temporal).reshape(normed.shape[0], 3 * width_here)
    grad_qkv = jnp.dot(normed.T, grad_mixed, preferred_element_type=jnp.float32).reshape(
        normed.shape[1], 3, width_here
    )
    grad_normed = jnp.dot(
        grad_mixed,
        w_qkv.reshape(w_qkv.shape[0], 3 * width_here).T,
        preferred_element_type=jnp.float32,
    )
    return (grad_qkv, grad_proj, grad_normed)


def attention_shards(qkv_shard, proj_shard):
    rows, parts, width = qkv_shard.shape
    return jnp.concatenate(
        [qkv_shard.astype(jnp.bfloat16).reshape(rows, parts * width), proj_shard.astype(jnp.bfloat16).T],
        axis=1,
    )


def gather_attention(mine, other, qkv_shape):
    rows, parts, width = qkv_shape
    split = parts * width
    qkv_local = jnp.stack(
        [mine[:, :split].reshape(rows, parts, width), other[:, :split].reshape(rows, parts, width)],
        axis=2,
    ).reshape(rows, 2 * split)
    proj_local = jnp.concatenate([mine[:, split:], other[:, split:]], axis=1)
    full = lax.all_gather(
        jnp.concatenate([qkv_local, proj_local], axis=1), "dp", axis=0, tiled=True
    )
    w_qkv = full[:, : 2 * split].reshape(full.shape[0], parts, 2 * width)
    w_proj = full[:, 2 * split :].T
    return w_qkv, w_proj


def mlp_shards(up_shard, down_shard):
    return jnp.concatenate([up_shard.astype(jnp.bfloat16), down_shard.astype(jnp.bfloat16).T], axis=1)


def gather_mlp(mine, other, width):
    local = jnp.concatenate(
        [mine[:, :width], other[:, :width], mine[:, width:], other[:, width:]], axis=1
    )
    full = lax.all_gather(local, "dp", axis=0, tiled=True)
    return full[:, : 2 * width], full[:, 2 * width :].T


def scatter_rows(pieces):
    flat = [p.reshape(p.shape[0], -1) for p in pieces]
    return lax.psum_scatter(
        jnp.concatenate(flat, axis=1).astype(jnp.bfloat16), "dp", scatter_dimension=0, tiled=True
    )


def finish_attention(local, qkv_shape, proj_shape):
    rows, parts, width = qkv_shape
    split = parts * 2 * width
    qkv = local[:, :split].reshape(rows, parts, 2, width)
    proj = local[:, split:]
    half = proj.shape[1] // 2
    mine = jnp.concatenate([qkv[:, :, 0].reshape(rows, -1), proj[:, :half]], axis=1)
    other = jnp.concatenate([qkv[:, :, 1].reshape(rows, -1), proj[:, half:]], axis=1)
    summed = mine.astype(jnp.float32) + swap_ty(other).astype(jnp.float32)
    return summed[:, : parts * width].reshape(qkv_shape), summed[:, parts * width :].T.reshape(proj_shape)


def finish_mlp(local, up_shape, down_shape):
    width = up_shape[1]
    mine = jnp.concatenate([local[:, :width], local[:, 2 * width : 3 * width]], axis=1)
    other = jnp.concatenate([local[:, width : 2 * width], local[:, 3 * width :]], axis=1)
    summed = mine.astype(jnp.float32) + swap_ty(other).astype(jnp.float32)
    return summed[:, :width].reshape(up_shape), summed[:, width:].T.reshape(down_shape)


def swap_ty(values):
    return lax.ppermute(values, "ty", perm=[(0, 1), (1, 0)])


def per_device(
    tokens,
    cotangent,
    norm_gains,
    qkv_time,
    proj_time,
    qkv_space,
    proj_space,
    up_weight,
    down_weight,
):
    time_mine = attention_shards(qkv_time, proj_time)
    time_qkv, time_proj = gather_attention(time_mine, swap_ty(time_mine), qkv_time.shape)
    later = jnp.concatenate(
        [attention_shards(qkv_space, proj_space), mlp_shards(up_weight, down_weight)], axis=1
    )
    later_other = swap_ty(later)
    cut = later.shape[1] - 2 * up_weight.shape[1]
    space_qkv, space_proj = gather_attention(later[:, :cut], later_other[:, :cut], qkv_space.shape)
    up_full, down_full = gather_mlp(later[:, cut:], later_other[:, cut:], up_weight.shape[1])

    def swap(values):
        return lax.ppermute(values, "core", perm=[(0, 1), (1, 0)])

    def spread_rows(values):
        return jnp.concatenate([values, swap(values)], axis=0)

    def sum_rows(values):
        half = values.shape[0] // 2
        return values[:half] + swap(values[half:].astype(jnp.bfloat16)).astype(jnp.float32)

    spread_grads = spread_rows
    sum_grads = sum_rows

    inputs = tokens.astype(jnp.float32)
    normed_time = spread_rows(normalize(inputs, norm_gains[0]).astype(jnp.bfloat16))
    grouped_time, summary_time, merged_time = attend_forward(normed_time, time_qkv, True)
    after_time = inputs + sum_rows(
        jnp.dot(merged_time, time_proj, preferred_element_type=jnp.float32)
    )
    normed_space = spread_rows(normalize(after_time, norm_gains[1]).astype(jnp.bfloat16))
    grouped_space, summary_space, merged_space = attend_forward(normed_space, space_qkv, False)
    after_space = after_time + sum_rows(
        jnp.dot(merged_space, space_proj, preferred_element_type=jnp.float32)
    )
    normed_mlp = spread_rows(normalize(after_space, norm_gains[2]).astype(jnp.bfloat16))
    hidden_pre = jnp.dot(normed_mlp, up_full, preferred_element_type=jnp.float32)
    hidden = jax.nn.gelu(hidden_pre, approximate=False).astype(jnp.bfloat16)
    output = (
        after_space + sum_rows(jnp.dot(hidden, down_full, preferred_element_type=jnp.float32))
    ).astype(jnp.bfloat16)

    grad_after = cotangent.astype(jnp.float32)
    down_rows = spread_grads(grad_after.astype(jnp.bfloat16))
    grad_down = jnp.dot(down_rows.T, hidden, preferred_element_type=jnp.float32)
    grad_hidden = jnp.dot(down_rows, down_full.T, preferred_element_type=jnp.float32)
    _, gelu_back = jax.vjp(partial(jax.nn.gelu, approximate=False), hidden_pre)
    grad_pre = gelu_back(grad_hidden)[0].astype(jnp.bfloat16)
    grad_up = jnp.dot(normed_mlp.T, grad_pre, preferred_element_type=jnp.float32)
    mlp_local = scatter_rows((grad_up, grad_down))
    grad_up, grad_down = finish_mlp(mlp_local, up_weight.shape, down_weight.shape)
    _, norm_back = jax.vjp(normalize, after_space, norm_gains[2])
    back_rows, gain_mlp = norm_back(
        sum_grads(jnp.dot(grad_pre, up_full.T, preferred_element_type=jnp.float32))
    )
    grad_after = grad_after + back_rows
    _, norm_back = jax.vjp(normalize, after_time, norm_gains[1])
    space_rows = spread_grads(grad_after.astype(jnp.bfloat16))
    grad_qkv_space, grad_proj_space, grad_normed = attend_backward(
        normed_space,
        space_qkv,
        space_proj,
        grouped_space,
        summary_space,
        merged_space,
        space_rows,
        False,
    )
    space_local = scatter_rows((grad_qkv_space, grad_proj_space))
    grad_qkv_space, grad_proj_space = finish_attention(space_local, qkv_space.shape, proj_space.shape)
    back_rows, gain_space = norm_back(sum_grads(grad_normed))
    grad_after = grad_after + back_rows
    time_rows = spread_grads(grad_after.astype(jnp.bfloat16))
    grad_qkv_time, grad_proj_time, grad_normed = attend_backward(
        normed_time, time_qkv, time_proj, grouped_time, summary_time, merged_time, time_rows, True
    )
    grad_qkv_time, grad_proj_time = finish_attention(
        scatter_rows((grad_qkv_time, grad_proj_time)), qkv_time.shape, proj_time.shape
    )
    _, norm_back = jax.vjp(normalize, inputs, norm_gains[0])
    back_rows, gain_time = norm_back(sum_grads(grad_normed))
    grad_tokens = grad_after + back_rows
    grad_gains = lax.psum(jnp.stack([gain_time, gain_space, gain_mlp]), ("dp", "ty", "core"))
    return (
        output,
        grad_tokens,
        grad_gains,
        grad_qkv_time,
        grad_proj_time,
        grad_qkv_space,
        grad_proj_space,
        grad_up,
        grad_down,
    )


def solution(mesh):
    def run(*args):
        rows_here = args[0].shape[0] // mesh.size
        cores = FRAMES * PATCH // rows_here
        tensor = mesh.shape["tensor"]
        assert tensor % cores == 0
        devices = mesh.devices.reshape(mesh.shape["dp"], tensor // cores, cores)
        chips = Mesh(devices, ("dp", "ty", "core"))
        rows = P(("dp", "ty", "core"), None)
        qkv = P("dp", None, ("ty", "core"))
        proj = P(("ty", "core"), "dp")
        up = P("dp", ("ty", "core"))
        down = P(("ty", "core"), "dp")
        mapped = jax.shard_map(
            per_device,
            mesh=chips,
            in_specs=(rows, rows, P(), qkv, proj, qkv, proj, up, down),
            out_specs=(rows, rows, P(), qkv, proj, qkv, proj, up, down),
            check_vma=False,
        )
        return mapped(*args)

    return run
```

```python
import math

import jax
import jax.numpy as jnp
from jax import lax
from jax.sharding import Mesh, PartitionSpec as P


HD = 64
FRAMES = 8
PATCH = 196


epsilon = 1e-06


def normalize(values, gain_row):
    center = values - jnp.mean(values, axis=-1, keepdims=True)
    spread = jnp.mean(center * center, axis=-1, keepdims=True)
    return center * lax.rsqrt(spread + epsilon) * gain_row


def to_groups(values, temporal):
    trailing = values.shape[1:]
    if temporal:
        clip_count = values.shape[0] // (FRAMES * PATCH)
        shaped = values.reshape((clip_count, FRAMES, PATCH) + trailing)
        shaped = jnp.swapaxes(shaped, 1, 2)
        return shaped.reshape((clip_count * PATCH, FRAMES) + trailing)
    return values.reshape((-1, PATCH) + trailing)


def from_groups(values, temporal):
    trailing = values.shape[2:]
    if temporal:
        clip_count = values.shape[0] // PATCH
        values = jnp.swapaxes(values.reshape((clip_count, PATCH, FRAMES) + trailing), 1, 2)
    return values.reshape((-1,) + trailing)


def attend_forward(normed, w_qkv, temporal):
    factor = 1.0 / math.sqrt(HD)
    width_here = w_qkv.shape[2]
    mixed_qkv = jnp.dot(
        normed, w_qkv.reshape(w_qkv.shape[0], 3 * width_here), preferred_element_type=jnp.float32
    )
    mixed_qkv = mixed_qkv.astype(jnp.bfloat16).reshape(normed.shape[0], 3, width_here // HD, HD)
    grouped = to_groups(mixed_qkv, temporal)
    scores = (
        jnp.einsum(
            "blhe,bmhe->bhlm",
            grouped[:, :, 0],
            grouped[:, :, 1],
            preferred_element_type=jnp.float32,
        )
        * factor
    )
    row_top = jnp.max(scores, axis=-1, keepdims=True)
    shifted = jnp.exp(scores - row_top)
    row_total = jnp.sum(shifted, axis=-1, keepdims=True)
    attn_probs = (shifted / row_total).astype(jnp.bfloat16)
    attended = jnp.einsum(
        "bhlm,bmhe->blhe", attn_probs, grouped[:, :, 2], preferred_element_type=jnp.float32
    )
    merged = from_groups(attended.astype(jnp.bfloat16), temporal).reshape(
        normed.shape[0], width_here
    )
    return (grouped, row_top + jnp.log(row_total), merged)


def attend_backward(normed, w_qkv, w_proj, grouped, summary, merged, grad_rows, temporal):
    factor = 1.0 / math.sqrt(HD)
    width_here = merged.shape[1]
    grad_proj = jnp.dot(grad_rows.T, merged, preferred_element_type=jnp.float32)
    grad_merged = jnp.dot(grad_rows, w_proj.T, preferred_element_type=jnp.float32).astype(
        jnp.bfloat16
    )
    grad_attended = to_groups(grad_merged.reshape(normed.shape[0], width_here // HD, HD), temporal)
    query_rows = grouped[:, :, 0]
    key_rows = grouped[:, :, 1]
    value_rows = grouped[:, :, 2]
    scores = (
        jnp.einsum("blhe,bmhe->bhlm", query_rows, key_rows, preferred_element_type=jnp.float32)
        * factor
    )
    attn_probs = jnp.exp(scores - summary)
    grad_value = jnp.einsum(
        "bhlm,blhe->bmhe",
        attn_probs.astype(jnp.bfloat16),
        grad_attended,
        preferred_element_type=jnp.float32,
    )
    grad_probs = jnp.einsum(
        "blhe,bmhe->bhlm", grad_attended, value_rows, preferred_element_type=jnp.float32
    )
    grad_scores = attn_probs * (
        grad_probs - jnp.sum(grad_probs * attn_probs, axis=-1, keepdims=True)
    )
    grad_scores = grad_scores.astype(jnp.bfloat16)
    grad_query = (
        jnp.einsum("bhlm,bmhe->blhe", grad_scores, key_rows, preferred_element_type=jnp.float32)
        * factor
    )
    grad_key = (
        jnp.einsum("bhlm,blhe->bmhe", grad_scores, query_rows, preferred_element_type=jnp.float32)
        * factor
    )
    stacked = jnp.stack([grad_query, grad_key, grad_value], axis=2).astype(jnp.bfloat16)
    grad_mixed = from_groups(stacked, temporal).reshape(normed.shape[0], 3 * width_here)
    grad_qkv = jnp.dot(normed.T, grad_mixed, preferred_element_type=jnp.float32).reshape(
        normed.shape[1], 3, width_here
    )
    grad_normed = jnp.dot(
        grad_mixed,
        w_qkv.reshape(w_qkv.shape[0], 3 * width_here).T,
        preferred_element_type=jnp.float32,
    )
    return (grad_qkv, grad_proj, grad_normed)


def attention_shards(qkv_shard, proj_shard):
    rows, parts, width = qkv_shard.shape
    return jnp.concatenate(
        [qkv_shard.astype(jnp.bfloat16).reshape(rows, parts * width), proj_shard.astype(jnp.bfloat16).T],
        axis=1,
    )


def gather_attention(mine, other, qkv_shape):
    rows, parts, width = qkv_shape
    split = parts * width
    qkv_local = jnp.stack(
        [mine[:, :split].reshape(rows, parts, width), other[:, :split].reshape(rows, parts, width)],
        axis=2,
    ).reshape(rows, 2 * split)
    proj_local = jnp.concatenate([mine[:, split:], other[:, split:]], axis=1)
    full = lax.all_gather(
        jnp.concatenate([qkv_local, proj_local], axis=1), "dp", axis=0, tiled=True
    )
    w_qkv = full[:, : 2 * split].reshape(full.shape[0], parts, 2 * width)
    w_proj = full[:, 2 * split :].T
    return w_qkv, w_proj


def mlp_shards(up_shard, down_shard):
    return jnp.concatenate([up_shard.astype(jnp.bfloat16), down_shard.astype(jnp.bfloat16).T], axis=1)


def gather_mlp(mine, other, width):
    local = jnp.concatenate(
        [mine[:, :width], other[:, :width], mine[:, width:], other[:, width:]], axis=1
    )
    full = lax.all_gather(local, "dp", axis=0, tiled=True)
    return full[:, : 2 * width], full[:, 2 * width :].T


def scatter_rows(pieces):
    flat = [p.reshape(p.shape[0], -1) for p in pieces]
    return lax.psum_scatter(
        jnp.concatenate(flat, axis=1).astype(jnp.bfloat16), "dp", scatter_dimension=0, tiled=True
    )


def finish_attention(local, qkv_shape, proj_shape):
    rows, parts, width = qkv_shape
    split = parts * 2 * width
    qkv = local[:, :split].reshape(rows, parts, 2, width)
    proj = local[:, split:]
    half = proj.shape[1] // 2
    mine = jnp.concatenate([qkv[:, :, 0].reshape(rows, -1), proj[:, :half]], axis=1)
    other = jnp.concatenate([qkv[:, :, 1].reshape(rows, -1), proj[:, half:]], axis=1)
    summed = mine.astype(jnp.float32) + swap_ty(other).astype(jnp.float32)
    return summed[:, : parts * width].reshape(qkv_shape), summed[:, parts * width :].T.reshape(proj_shape)


def finish_mlp(local, up_shape, down_shape):
    width = up_shape[1]
    mine = jnp.concatenate([local[:, :width], local[:, 2 * width : 3 * width]], axis=1)
    other = jnp.concatenate([local[:, width : 2 * width], local[:, 3 * width :]], axis=1)
    summed = mine.astype(jnp.float32) + swap_ty(other).astype(jnp.float32)
    return summed[:, :width].reshape(up_shape), summed[:, width:].T.reshape(down_shape)


def swap_ty(values):
    return lax.ppermute(values, "ty", perm=[(0, 1), (1, 0)])


def per_device(
    tokens,
    cotangent,
    norm_gains,
    qkv_time,
    proj_time,
    qkv_space,
    proj_space,
    up_weight,
    down_weight,
):
    time_mine = attention_shards(qkv_time, proj_time)
    time_qkv, time_proj = gather_attention(time_mine, swap_ty(time_mine), qkv_time.shape)
    later = jnp.concatenate(
        [attention_shards(qkv_space, proj_space), mlp_shards(up_weight, down_weight)], axis=1
    )
    later_other = swap_ty(later)
    cut = later.shape[1] - 2 * up_weight.shape[1]
    space_qkv, space_proj = gather_attention(later[:, :cut], later_other[:, :cut], qkv_space.shape)
    up_full, down_full = gather_mlp(later[:, cut:], later_other[:, cut:], up_weight.shape[1])

    def swap(values):
        return lax.ppermute(values, "core", perm=[(0, 1), (1, 0)])

    def spread_rows(values):
        return jnp.concatenate([values, swap(values)], axis=0)

    def sum_rows(values):
        half = values.shape[0] // 2
        return values[:half] + swap(values[half:].astype(jnp.bfloat16)).astype(jnp.float32)

    spread_grads = spread_rows
    sum_grads = sum_rows

    inputs = tokens.astype(jnp.float32)
    normed_time = spread_rows(normalize(inputs, norm_gains[0]).astype(jnp.bfloat16))
    grouped_time, summary_time, merged_time = attend_forward(normed_time, time_qkv, True)
    after_time = inputs + sum_rows(
        jnp.dot(merged_time, time_proj, preferred_element_type=jnp.float32)
    )
    normed_space = spread_rows(normalize(after_time, norm_gains[1]).astype(jnp.bfloat16))
    grouped_space, summary_space, merged_space = attend_forward(normed_space, space_qkv, False)
    after_space = after_time + sum_rows(
        jnp.dot(merged_space, space_proj, preferred_element_type=jnp.float32)
    )
    normed_mlp = spread_rows(normalize(after_space, norm_gains[2]).astype(jnp.bfloat16))
    hidden_pre = jnp.dot(normed_mlp, up_full, preferred_element_type=jnp.float32)
    half_cdf = 0.5 * lax.erfc(-hidden_pre * math.sqrt(0.5))
    hidden = (hidden_pre * half_cdf).astype(jnp.bfloat16)
    gelu_slope = half_cdf + hidden_pre * jnp.exp(-0.5 * hidden_pre * hidden_pre) * (
        1.0 / math.sqrt(2.0 * math.pi)
    )
    output = (
        after_space + sum_rows(jnp.dot(hidden, down_full, preferred_element_type=jnp.float32))
    ).astype(jnp.bfloat16)

    grad_after = cotangent.astype(jnp.float32)
    down_rows = spread_grads(grad_after.astype(jnp.bfloat16))
    grad_down = jnp.dot(down_rows.T, hidden, preferred_element_type=jnp.float32)
    grad_hidden = jnp.dot(down_rows, down_full.T, preferred_element_type=jnp.float32)
    grad_pre = (grad_hidden * gelu_slope).astype(jnp.bfloat16)
    grad_up = jnp.dot(normed_mlp.T, grad_pre, preferred_element_type=jnp.float32)
    mlp_local = scatter_rows((grad_up, grad_down))
    grad_up, grad_down = finish_mlp(mlp_local, up_weight.shape, down_weight.shape)
    _, norm_back = jax.vjp(normalize, after_space, norm_gains[2])
    back_rows, gain_mlp = norm_back(
        sum_grads(jnp.dot(grad_pre, up_full.T, preferred_element_type=jnp.float32))
    )
    grad_after = grad_after + back_rows
    _, norm_back = jax.vjp(normalize, after_time, norm_gains[1])
    space_rows = spread_grads(grad_after.astype(jnp.bfloat16))
    grad_qkv_space, grad_proj_space, grad_normed = attend_backward(
        normed_space,
        space_qkv,
        space_proj,
        grouped_space,
        summary_space,
        merged_space,
        space_rows,
        False,
    )
    space_local = scatter_rows((grad_qkv_space, grad_proj_space))
    grad_qkv_space, grad_proj_space = finish_attention(space_local, qkv_space.shape, proj_space.shape)
    back_rows, gain_space = norm_back(sum_grads(grad_normed))
    grad_after = grad_after + back_rows
    time_rows = spread_grads(grad_after.astype(jnp.bfloat16))
    grad_qkv_time, grad_proj_time, grad_normed = attend_backward(
        normed_time, time_qkv, time_proj, grouped_time, summary_time, merged_time, time_rows, True
    )
    grad_qkv_time, grad_proj_time = finish_attention(
        scatter_rows((grad_qkv_time, grad_proj_time)), qkv_time.shape, proj_time.shape
    )
    _, norm_back = jax.vjp(normalize, inputs, norm_gains[0])
    back_rows, gain_time = norm_back(sum_grads(grad_normed))
    grad_tokens = grad_after + back_rows
    grad_gains = lax.psum(jnp.stack([gain_time, gain_space, gain_mlp]), ("dp", "ty", "core"))
    return (
        output,
        grad_tokens,
        grad_gains,
        grad_qkv_time,
        grad_proj_time,
        grad_qkv_space,
        grad_proj_space,
        grad_up,
        grad_down,
    )


def solution(mesh):
    def run(*args):
        rows_here = args[0].shape[0] // mesh.size
        cores = FRAMES * PATCH // rows_here
        tensor = mesh.shape["tensor"]
        assert tensor % cores == 0
        devices = mesh.devices.reshape(mesh.shape["dp"], tensor // cores, cores)
        chips = Mesh(devices, ("dp", "ty", "core"))
        rows = P(("dp", "ty", "core"), None)
        qkv = P("dp", None, ("ty", "core"))
        proj = P(("ty", "core"), "dp")
        up = P("dp", ("ty", "core"))
        down = P(("ty", "core"), "dp")
        mapped = jax.shard_map(
            per_device,
            mesh=chips,
            in_specs=(rows, rows, P(), qkv, proj, qkv, proj, up, down),
            out_specs=(rows, rows, P(), qkv, proj, qkv, proj, up, down),
            check_vma=False,
        )
        return mapped(*args)

    return run
```

```python
from functools import partial
import math

import jax
import jax.numpy as jnp
from jax import lax
from jax.sharding import Mesh, PartitionSpec as P


HD = 64
FRAMES = 8
PATCH = 196


epsilon = 1e-06


def normalize(values, gain_row):
    center = values - jnp.mean(values, axis=-1, keepdims=True)
    spread = jnp.mean(center * center, axis=-1, keepdims=True)
    return center * lax.rsqrt(spread + epsilon) * gain_row


def to_groups(values, temporal):
    trailing = values.shape[1:]
    if temporal:
        clip_count = values.shape[0] // (FRAMES * PATCH)
        shaped = values.reshape((clip_count, FRAMES, PATCH) + trailing)
        shaped = jnp.swapaxes(shaped, 1, 2)
        return shaped.reshape((clip_count * PATCH, FRAMES) + trailing)
    return values.reshape((-1, PATCH) + trailing)


def from_groups(values, temporal):
    trailing = values.shape[2:]
    if temporal:
        clip_count = values.shape[0] // PATCH
        values = jnp.swapaxes(values.reshape((clip_count, PATCH, FRAMES) + trailing), 1, 2)
    return values.reshape((-1,) + trailing)


def attend_forward(normed, w_qkv, temporal):
    factor = 1.0 / math.sqrt(HD)
    width_here = w_qkv.shape[2]
    mixed_qkv = jnp.dot(
        normed, w_qkv.reshape(w_qkv.shape[0], 3 * width_here), preferred_element_type=jnp.float32
    )
    mixed_qkv = mixed_qkv.astype(jnp.bfloat16).reshape(normed.shape[0], 3, width_here // HD, HD)
    grouped = to_groups(mixed_qkv, temporal)
    scores = (
        jnp.einsum(
            "blhe,bmhe->bhlm",
            grouped[:, :, 0],
            grouped[:, :, 1],
            preferred_element_type=jnp.float32,
        )
        * factor
    )
    row_top = jnp.max(scores, axis=-1, keepdims=True)
    shifted = jnp.exp(scores - row_top)
    row_total = jnp.sum(shifted, axis=-1, keepdims=True)
    attn_probs = (shifted / row_total).astype(jnp.bfloat16)
    attended = jnp.einsum(
        "bhlm,bmhe->blhe", attn_probs, grouped[:, :, 2], preferred_element_type=jnp.float32
    )
    merged = from_groups(attended.astype(jnp.bfloat16), temporal).reshape(
        normed.shape[0], width_here
    )
    return (grouped, row_top + jnp.log(row_total), merged)


def attend_backward(normed, w_qkv, w_proj, grouped, summary, merged, grad_rows, temporal):
    factor = 1.0 / math.sqrt(HD)
    width_here = merged.shape[1]
    grad_proj = jnp.dot(grad_rows.T, merged, preferred_element_type=jnp.float32)
    grad_merged = jnp.dot(grad_rows, w_proj.T, preferred_element_type=jnp.float32).astype(
        jnp.bfloat16
    )
    grad_attended = to_groups(grad_merged.reshape(normed.shape[0], width_here // HD, HD), temporal)
    query_rows = grouped[:, :, 0]
    key_rows = grouped[:, :, 1]
    value_rows = grouped[:, :, 2]
    scores = (
        jnp.einsum("blhe,bmhe->bhlm", query_rows, key_rows, preferred_element_type=jnp.float32)
        * factor
    )
    attn_probs = jnp.exp(scores - summary)
    grad_value = jnp.einsum(
        "bhlm,blhe->bmhe",
        attn_probs.astype(jnp.bfloat16),
        grad_attended,
        preferred_element_type=jnp.float32,
    )
    grad_probs = jnp.einsum(
        "blhe,bmhe->bhlm", grad_attended, value_rows, preferred_element_type=jnp.float32
    )
    grad_scores = attn_probs * (
        grad_probs - jnp.sum(grad_probs * attn_probs, axis=-1, keepdims=True)
    )
    grad_scores = grad_scores.astype(jnp.bfloat16)
    grad_query = (
        jnp.einsum("bhlm,bmhe->blhe", grad_scores, key_rows, preferred_element_type=jnp.float32)
        * factor
    )
    grad_key = (
        jnp.einsum("bhlm,blhe->bmhe", grad_scores, query_rows, preferred_element_type=jnp.float32)
        * factor
    )
    stacked = jnp.stack([grad_query, grad_key, grad_value], axis=2).astype(jnp.bfloat16)
    grad_mixed = from_groups(stacked, temporal).reshape(normed.shape[0], 3 * width_here)
    grad_qkv = jnp.dot(normed.T, grad_mixed, preferred_element_type=jnp.float32).reshape(
        normed.shape[1], 3, width_here
    )
    grad_normed = jnp.dot(
        grad_mixed,
        w_qkv.reshape(w_qkv.shape[0], 3 * width_here).T,
        preferred_element_type=jnp.float32,
    )
    return (grad_qkv, grad_proj, grad_normed)


def attention_shards(qkv_shard, proj_shard):
    rows, parts, width = qkv_shard.shape
    return jnp.concatenate(
        [qkv_shard.astype(jnp.bfloat16).reshape(rows, parts * width), proj_shard.astype(jnp.bfloat16).T],
        axis=1,
    )


def gather_attention(mine, other, qkv_shape):
    rows, parts, width = qkv_shape
    split = parts * width
    qkv_local = jnp.stack(
        [mine[:, :split].reshape(rows, parts, width), other[:, :split].reshape(rows, parts, width)],
        axis=2,
    ).reshape(rows, 2 * split)
    proj_local = jnp.concatenate([mine[:, split:], other[:, split:]], axis=1)
    full = lax.all_gather(
        jnp.concatenate([qkv_local, proj_local], axis=1), "dp", axis=0, tiled=True
    )
    w_qkv = full[:, : 2 * split].reshape(full.shape[0], parts, 2 * width)
    w_proj = full[:, 2 * split :].T
    return w_qkv, w_proj


def mlp_shards(up_shard, down_shard):
    return jnp.concatenate([up_shard.astype(jnp.bfloat16), down_shard.astype(jnp.bfloat16).T], axis=1)


def gather_mlp(mine, other, width):
    local = jnp.concatenate(
        [mine[:, :width], other[:, :width], mine[:, width:], other[:, width:]], axis=1
    )
    full = ring_gather(local)
    return full[:, : 2 * width], full[:, 2 * width :].T


DP_RING = (0, 2, 4, 6, 7, 5, 3, 1)


def ring_gather(local):
    count = lax.axis_size("dp")
    if count != len(DP_RING):
        return lax.all_gather(local, "dp", axis=0, tiled=True)
    ring = jnp.array(DP_RING, jnp.int32)
    place = jnp.array([DP_RING.index(d) for d in range(count)], jnp.int32)
    forward = [(DP_RING[i], DP_RING[(i + 1) % count]) for i in range(count)]
    backward = [(DP_RING[(i + 1) % count], DP_RING[i]) for i in range(count)]
    here = place[lax.axis_index("dp")]
    blocks = [local]
    owners = [ring[here]]
    ahead = behind = local
    for step in range(1, count // 2 + 1):
        ahead = lax.ppermute(ahead, "dp", forward)
        blocks.append(ahead)
        owners.append(ring[(here - step) % count])
        if step < count - count // 2:
            behind = lax.ppermute(behind, "dp", backward)
            blocks.append(behind)
            owners.append(ring[(here + step) % count])
    order = jnp.zeros((count,), jnp.int32).at[jnp.stack(owners)].set(jnp.arange(count, dtype=jnp.int32))
    stacked = jnp.stack(blocks)
    return jnp.take(stacked, order, axis=0).reshape(count * local.shape[0], local.shape[1])


def scatter_rows(pieces):
    flat = [p.reshape(p.shape[0], -1) for p in pieces]
    return lax.psum_scatter(
        jnp.concatenate(flat, axis=1).astype(jnp.bfloat16), "dp", scatter_dimension=0, tiled=True
    )


def finish_attention(local, qkv_shape, proj_shape):
    rows, parts, width = qkv_shape
    split = parts * 2 * width
    qkv = local[:, :split].reshape(rows, parts, 2, width)
    proj = local[:, split:]
    half = proj.shape[1] // 2
    mine = jnp.concatenate([qkv[:, :, 0].reshape(rows, -1), proj[:, :half]], axis=1)
    other = jnp.concatenate([qkv[:, :, 1].reshape(rows, -1), proj[:, half:]], axis=1)
    summed = mine.astype(jnp.float32) + swap_ty(other).astype(jnp.float32)
    return summed[:, : parts * width].reshape(qkv_shape), summed[:, parts * width :].T.reshape(proj_shape)


def finish_mlp(local, up_shape, down_shape):
    width = up_shape[1]
    mine = jnp.concatenate([local[:, :width], local[:, 2 * width : 3 * width]], axis=1)
    other = jnp.concatenate([local[:, width : 2 * width], local[:, 3 * width :]], axis=1)
    summed = mine.astype(jnp.float32) + swap_ty(other).astype(jnp.float32)
    return summed[:, :width].reshape(up_shape), summed[:, width:].T.reshape(down_shape)


def swap_ty(values):
    return lax.ppermute(values, "ty", perm=[(0, 1), (1, 0)])


def per_device(
    tokens,
    cotangent,
    norm_gains,
    qkv_time,
    proj_time,
    qkv_space,
    proj_space,
    up_weight,
    down_weight,
):
    time_mine = attention_shards(qkv_time, proj_time)
    time_qkv, time_proj = gather_attention(time_mine, swap_ty(time_mine), qkv_time.shape)
    later = jnp.concatenate(
        [attention_shards(qkv_space, proj_space), mlp_shards(up_weight, down_weight)], axis=1
    )
    later_other = swap_ty(later)
    cut = later.shape[1] - 2 * up_weight.shape[1]
    space_qkv, space_proj = gather_attention(later[:, :cut], later_other[:, :cut], qkv_space.shape)
    up_full, down_full = gather_mlp(later[:, cut:], later_other[:, cut:], up_weight.shape[1])

    def swap(values):
        return lax.ppermute(values, "core", perm=[(0, 1), (1, 0)])

    def spread_rows(values):
        return jnp.concatenate([values, swap(values)], axis=0)

    def sum_rows(values):
        half = values.shape[0] // 2
        return values[:half] + swap(values[half:].astype(jnp.bfloat16)).astype(jnp.float32)

    spread_grads = spread_rows
    sum_grads = sum_rows

    inputs = tokens.astype(jnp.float32)
    normed_time = spread_rows(normalize(inputs, norm_gains[0]).astype(jnp.bfloat16))
    grouped_time, summary_time, merged_time = attend_forward(normed_time, time_qkv, True)
    after_time = inputs + sum_rows(
        jnp.dot(merged_time, time_proj, preferred_element_type=jnp.float32)
    )
    normed_space = spread_rows(normalize(after_time, norm_gains[1]).astype(jnp.bfloat16))
    grouped_space, summary_space, merged_space = attend_forward(normed_space, space_qkv, False)
    after_space = after_time + sum_rows(
        jnp.dot(merged_space, space_proj, preferred_element_type=jnp.float32)
    )
    normed_mlp = spread_rows(normalize(after_space, norm_gains[2]).astype(jnp.bfloat16))
    hidden_pre = jnp.dot(normed_mlp, up_full, preferred_element_type=jnp.float32)
    hidden = jax.nn.gelu(hidden_pre, approximate=False).astype(jnp.bfloat16)
    output = (
        after_space + sum_rows(jnp.dot(hidden, down_full, preferred_element_type=jnp.float32))
    ).astype(jnp.bfloat16)

    grad_after = cotangent.astype(jnp.float32)
    down_rows = spread_grads(grad_after.astype(jnp.bfloat16))
    grad_down = jnp.dot(down_rows.T, hidden, preferred_element_type=jnp.float32)
    grad_hidden = jnp.dot(down_rows, down_full.T, preferred_element_type=jnp.float32)
    _, gelu_back = jax.vjp(partial(jax.nn.gelu, approximate=False), hidden_pre)
    grad_pre = gelu_back(grad_hidden)[0].astype(jnp.bfloat16)
    grad_up = jnp.dot(normed_mlp.T, grad_pre, preferred_element_type=jnp.float32)
    mlp_local = scatter_rows((grad_up, grad_down))
    grad_up, grad_down = finish_mlp(mlp_local, up_weight.shape, down_weight.shape)
    _, norm_back = jax.vjp(normalize, after_space, norm_gains[2])
    back_rows, gain_mlp = norm_back(
        sum_grads(jnp.dot(grad_pre, up_full.T, preferred_element_type=jnp.float32))
    )
    grad_after = grad_after + back_rows
    _, norm_back = jax.vjp(normalize, after_time, norm_gains[1])
    space_rows = spread_grads(grad_after.astype(jnp.bfloat16))
    grad_qkv_space, grad_proj_space, grad_normed = attend_backward(
        normed_space,
        space_qkv,
        space_proj,
        grouped_space,
        summary_space,
        merged_space,
        space_rows,
        False,
    )
    space_local = scatter_rows((grad_qkv_space, grad_proj_space))
    grad_qkv_space, grad_proj_space = finish_attention(space_local, qkv_space.shape, proj_space.shape)
    back_rows, gain_space = norm_back(sum_grads(grad_normed))
    grad_after = grad_after + back_rows
    time_rows = spread_grads(grad_after.astype(jnp.bfloat16))
    grad_qkv_time, grad_proj_time, grad_normed = attend_backward(
        normed_time, time_qkv, time_proj, grouped_time, summary_time, merged_time, time_rows, True
    )
    grad_qkv_time, grad_proj_time = finish_attention(
        scatter_rows((grad_qkv_time, grad_proj_time)), qkv_time.shape, proj_time.shape
    )
    _, norm_back = jax.vjp(normalize, inputs, norm_gains[0])
    back_rows, gain_time = norm_back(sum_grads(grad_normed))
    grad_tokens = grad_after + back_rows
    grad_gains = lax.psum(jnp.stack([gain_time, gain_space, gain_mlp]), ("dp", "ty", "core"))
    return (
        output,
        grad_tokens,
        grad_gains,
        grad_qkv_time,
        grad_proj_time,
        grad_qkv_space,
        grad_proj_space,
        grad_up,
        grad_down,
    )


def solution(mesh):
    def run(*args):
        rows_here = args[0].shape[0] // mesh.size
        cores = FRAMES * PATCH // rows_here
        tensor = mesh.shape["tensor"]
        assert tensor % cores == 0
        devices = mesh.devices.reshape(mesh.shape["dp"], tensor // cores, cores)
        chips = Mesh(devices, ("dp", "ty", "core"))
        rows = P(("dp", "ty", "core"), None)
        qkv = P("dp", None, ("ty", "core"))
        proj = P(("ty", "core"), "dp")
        up = P("dp", ("ty", "core"))
        down = P(("ty", "core"), "dp")
        mapped = jax.shard_map(
            per_device,
            mesh=chips,
            in_specs=(rows, rows, P(), qkv, proj, qkv, proj, up, down),
            out_specs=(rows, rows, P(), qkv, proj, qkv, proj, up, down),
            check_vma=False,
        )
        return mapped(*args)

    return run
```

```python
from functools import partial
import math

import jax
import jax.numpy as jnp
from jax import lax
from jax.sharding import Mesh, PartitionSpec as P


HD = 64
FRAMES = 8
PATCH = 196


epsilon = 1e-06


def normalize(values, gain_row):
    center = values - jnp.mean(values, axis=-1, keepdims=True)
    spread = jnp.mean(center * center, axis=-1, keepdims=True)
    return center * lax.rsqrt(spread + epsilon) * gain_row


def to_groups(values, temporal):
    trailing = values.shape[1:]
    if temporal:
        clip_count = values.shape[0] // (FRAMES * PATCH)
        shaped = values.reshape((clip_count, FRAMES, PATCH) + trailing)
        shaped = jnp.swapaxes(shaped, 1, 2)
        return shaped.reshape((clip_count * PATCH, FRAMES) + trailing)
    return values.reshape((-1, PATCH) + trailing)


def from_groups(values, temporal):
    trailing = values.shape[2:]
    if temporal:
        clip_count = values.shape[0] // PATCH
        values = jnp.swapaxes(values.reshape((clip_count, PATCH, FRAMES) + trailing), 1, 2)
    return values.reshape((-1,) + trailing)


def attend_forward(normed, w_qkv, temporal):
    factor = 1.0 / math.sqrt(HD)
    width_here = w_qkv.shape[2]
    mixed_qkv = jnp.dot(
        normed, w_qkv.reshape(w_qkv.shape[0], 3 * width_here), preferred_element_type=jnp.float32
    )
    mixed_qkv = mixed_qkv.astype(jnp.bfloat16).reshape(normed.shape[0], 3, width_here // HD, HD)
    grouped = to_groups(mixed_qkv, temporal)
    scores = (
        jnp.einsum(
            "blhe,bmhe->bhlm",
            grouped[:, :, 0],
            grouped[:, :, 1],
            preferred_element_type=jnp.float32,
        )
        * factor
    )
    row_top = jnp.max(scores, axis=-1, keepdims=True)
    shifted = jnp.exp(scores - row_top)
    row_total = jnp.sum(shifted, axis=-1, keepdims=True)
    attn_probs = (shifted / row_total).astype(jnp.bfloat16)
    attended = jnp.einsum(
        "bhlm,bmhe->blhe", attn_probs, grouped[:, :, 2], preferred_element_type=jnp.float32
    )
    merged = from_groups(attended.astype(jnp.bfloat16), temporal).reshape(
        normed.shape[0], width_here
    )
    return (grouped, row_top + jnp.log(row_total), merged)


def attend_backward(normed, w_qkv, w_proj, grouped, summary, merged, grad_rows, temporal):
    factor = 1.0 / math.sqrt(HD)
    width_here = merged.shape[1]
    grad_proj = jnp.dot(grad_rows.T, merged, preferred_element_type=jnp.float32)
    grad_merged = jnp.dot(grad_rows, w_proj.T, preferred_element_type=jnp.float32).astype(
        jnp.bfloat16
    )
    grad_attended = to_groups(grad_merged.reshape(normed.shape[0], width_here // HD, HD), temporal)
    query_rows = grouped[:, :, 0]
    key_rows = grouped[:, :, 1]
    value_rows = grouped[:, :, 2]
    scores = (
        jnp.einsum("blhe,bmhe->bhlm", query_rows, key_rows, preferred_element_type=jnp.float32)
        * factor
    )
    attn_probs = jnp.exp(scores - summary)
    grad_value = jnp.einsum(
        "bhlm,blhe->bmhe",
        attn_probs.astype(jnp.bfloat16),
        grad_attended,
        preferred_element_type=jnp.float32,
    )
    grad_probs = jnp.einsum(
        "blhe,bmhe->bhlm", grad_attended, value_rows, preferred_element_type=jnp.float32
    )
    grad_scores = attn_probs * (
        grad_probs - jnp.sum(grad_probs * attn_probs, axis=-1, keepdims=True)
    )
    grad_scores = grad_scores.astype(jnp.bfloat16)
    grad_query = (
        jnp.einsum("bhlm,bmhe->blhe", grad_scores, key_rows, preferred_element_type=jnp.float32)
        * factor
    )
    grad_key = (
        jnp.einsum("bhlm,blhe->bmhe", grad_scores, query_rows, preferred_element_type=jnp.float32)
        * factor
    )
    stacked = jnp.stack([grad_query, grad_key, grad_value], axis=2).astype(jnp.bfloat16)
    grad_mixed = from_groups(stacked, temporal).reshape(normed.shape[0], 3 * width_here)
    grad_qkv = jnp.dot(normed.T, grad_mixed, preferred_element_type=jnp.float32).reshape(
        normed.shape[1], 3, width_here
    )
    grad_normed = jnp.dot(
        grad_mixed,
        w_qkv.reshape(w_qkv.shape[0], 3 * width_here).T,
        preferred_element_type=jnp.float32,
    )
    return (grad_qkv, grad_proj, grad_normed)


def attention_shards(qkv_shard, proj_shard):
    rows, parts, width = qkv_shard.shape
    return jnp.concatenate(
        [qkv_shard.astype(jnp.bfloat16).reshape(rows, parts * width), proj_shard.astype(jnp.bfloat16).T],
        axis=1,
    )


def gather_attention(mine, other, qkv_shape):
    rows, parts, width = qkv_shape
    split = parts * width
    qkv_local = jnp.stack(
        [mine[:, :split].reshape(rows, parts, width), other[:, :split].reshape(rows, parts, width)],
        axis=2,
    ).reshape(rows, 2 * split)
    proj_local = jnp.concatenate([mine[:, split:], other[:, split:]], axis=1)
    full = lax.all_gather(
        jnp.concatenate([qkv_local, proj_local], axis=1), "dp", axis=0, tiled=True
    )
    w_qkv = full[:, : 2 * split].reshape(full.shape[0], parts, 2 * width)
    w_proj = full[:, 2 * split :].T
    return w_qkv, w_proj


def mlp_shards(up_shard, down_shard):
    return jnp.concatenate([up_shard.astype(jnp.bfloat16), down_shard.astype(jnp.bfloat16).T], axis=1)


def gather_mlp(mine, other, width):
    up = lax.all_gather(
        jnp.concatenate([mine[:, :width], other[:, :width]], axis=1), "dp", axis=0, tiled=True
    )
    down = lax.all_gather(
        jnp.concatenate([mine[:, width:], other[:, width:]], axis=1), "dp", axis=0, tiled=True
    )
    return up, down.T


def scatter_rows(pieces):
    flat = [p.reshape(p.shape[0], -1) for p in pieces]
    return lax.psum_scatter(
        jnp.concatenate(flat, axis=1).astype(jnp.bfloat16), "dp", scatter_dimension=0, tiled=True
    )


def finish_attention(local, qkv_shape, proj_shape):
    rows, parts, width = qkv_shape
    split = parts * 2 * width
    qkv = local[:, :split].reshape(rows, parts, 2, width)
    proj = local[:, split:]
    half = proj.shape[1] // 2
    mine = jnp.concatenate([qkv[:, :, 0].reshape(rows, -1), proj[:, :half]], axis=1)
    other = jnp.concatenate([qkv[:, :, 1].reshape(rows, -1), proj[:, half:]], axis=1)
    summed = mine.astype(jnp.float32) + swap_ty(other).astype(jnp.float32)
    return summed[:, : parts * width].reshape(qkv_shape), summed[:, parts * width :].T.reshape(proj_shape)


def finish_mlp(local, up_shape, down_shape):
    width = up_shape[1]
    mine = jnp.concatenate([local[:, :width], local[:, 2 * width : 3 * width]], axis=1)
    other = jnp.concatenate([local[:, width : 2 * width], local[:, 3 * width :]], axis=1)
    summed = mine.astype(jnp.float32) + swap_ty(other).astype(jnp.float32)
    return summed[:, :width].reshape(up_shape), summed[:, width:].T.reshape(down_shape)


def swap_ty(values):
    return lax.ppermute(values, "ty", perm=[(0, 1), (1, 0)])


def per_device(
    tokens,
    cotangent,
    norm_gains,
    qkv_time,
    proj_time,
    qkv_space,
    proj_space,
    up_weight,
    down_weight,
):
    time_mine = attention_shards(qkv_time, proj_time)
    time_qkv, time_proj = gather_attention(time_mine, swap_ty(time_mine), qkv_time.shape)
    later = jnp.concatenate(
        [attention_shards(qkv_space, proj_space), mlp_shards(up_weight, down_weight)], axis=1
    )
    later_other = swap_ty(later)
    cut = later.shape[1] - 2 * up_weight.shape[1]
    space_qkv, space_proj = gather_attention(later[:, :cut], later_other[:, :cut], qkv_space.shape)
    up_full, down_full = gather_mlp(later[:, cut:], later_other[:, cut:], up_weight.shape[1])

    def swap(values):
        return lax.ppermute(values, "core", perm=[(0, 1), (1, 0)])

    def spread_rows(values):
        return jnp.concatenate([values, swap(values)], axis=0)

    def sum_rows(values):
        half = values.shape[0] // 2
        return values[:half] + swap(values[half:].astype(jnp.bfloat16)).astype(jnp.float32)

    spread_grads = spread_rows
    sum_grads = sum_rows

    inputs = tokens.astype(jnp.float32)
    normed_time = spread_rows(normalize(inputs, norm_gains[0]).astype(jnp.bfloat16))
    grouped_time, summary_time, merged_time = attend_forward(normed_time, time_qkv, True)
    after_time = inputs + sum_rows(
        jnp.dot(merged_time, time_proj, preferred_element_type=jnp.float32)
    )
    normed_space = spread_rows(normalize(after_time, norm_gains[1]).astype(jnp.bfloat16))
    grouped_space, summary_space, merged_space = attend_forward(normed_space, space_qkv, False)
    after_space = after_time + sum_rows(
        jnp.dot(merged_space, space_proj, preferred_element_type=jnp.float32)
    )
    normed_mlp = spread_rows(normalize(after_space, norm_gains[2]).astype(jnp.bfloat16))
    hidden_pre = jnp.dot(normed_mlp, up_full, preferred_element_type=jnp.float32)
    hidden = jax.nn.gelu(hidden_pre, approximate=False).astype(jnp.bfloat16)

    grad_after = cotangent.astype(jnp.float32)
    down_rows = spread_grads(grad_after.astype(jnp.bfloat16))
    grad_down = jnp.dot(down_rows.T, hidden, preferred_element_type=jnp.float32)
    grad_hidden = jnp.dot(down_rows, down_full.T, preferred_element_type=jnp.float32)
    _, gelu_back = jax.vjp(partial(jax.nn.gelu, approximate=False), hidden_pre)
    grad_pre = gelu_back(grad_hidden)[0].astype(jnp.bfloat16)
    grad_up = jnp.dot(normed_mlp.T, grad_pre, preferred_element_type=jnp.float32)
    mlp_local = scatter_rows((grad_up, grad_down))
    grad_up, grad_down = finish_mlp(mlp_local, up_weight.shape, down_weight.shape)
    _, norm_back = jax.vjp(normalize, after_space, norm_gains[2])
    back_rows, gain_mlp = norm_back(
        sum_grads(jnp.dot(grad_pre, up_full.T, preferred_element_type=jnp.float32))
    )
    grad_after = grad_after + back_rows
    _, norm_back = jax.vjp(normalize, after_time, norm_gains[1])
    space_rows = spread_grads(grad_after.astype(jnp.bfloat16))
    grad_qkv_space, grad_proj_space, grad_normed = attend_backward(
        normed_space,
        space_qkv,
        space_proj,
        grouped_space,
        summary_space,
        merged_space,
        space_rows,
        False,
    )
    space_local = scatter_rows((grad_qkv_space, grad_proj_space))
    grad_qkv_space, grad_proj_space = finish_attention(space_local, qkv_space.shape, proj_space.shape)
    back_rows, gain_space = norm_back(sum_grads(grad_normed))
    grad_after = grad_after + back_rows
    time_rows = spread_grads(grad_after.astype(jnp.bfloat16))
    grad_qkv_time, grad_proj_time, grad_normed = attend_backward(
        normed_time, time_qkv, time_proj, grouped_time, summary_time, merged_time, time_rows, True
    )
    time_local = scatter_rows((grad_qkv_time, grad_proj_time))
    late_hidden, late_rows, _ = lax.optimization_barrier((hidden, after_space, grad_qkv_time))
    output = (
        late_rows
        + sum_rows(jnp.dot(late_hidden, down_full, preferred_element_type=jnp.float32))
    ).astype(jnp.bfloat16)
    grad_qkv_time, grad_proj_time = finish_attention(time_local, qkv_time.shape, proj_time.shape)
    _, norm_back = jax.vjp(normalize, inputs, norm_gains[0])
    back_rows, gain_time = norm_back(sum_grads(grad_normed))
    grad_tokens = grad_after + back_rows
    grad_gains = lax.psum(jnp.stack([gain_time, gain_space, gain_mlp]), ("dp", "ty", "core"))
    return (
        output,
        grad_tokens,
        grad_gains,
        grad_qkv_time,
        grad_proj_time,
        grad_qkv_space,
        grad_proj_space,
        grad_up,
        grad_down,
    )


def solution(mesh):
    def run(*args):
        rows_here = args[0].shape[0] // mesh.size
        cores = FRAMES * PATCH // rows_here
        tensor = mesh.shape["tensor"]
        assert tensor % cores == 0
        devices = mesh.devices.reshape(mesh.shape["dp"], tensor // cores, cores)
        chips = Mesh(devices, ("dp", "ty", "core"))
        rows = P(("dp", "ty", "core"), None)
        qkv = P("dp", None, ("ty", "core"))
        proj = P(("ty", "core"), "dp")
        up = P("dp", ("ty", "core"))
        down = P(("ty", "core"), "dp")
        mapped = jax.shard_map(
            per_device,
            mesh=chips,
            in_specs=(rows, rows, P(), qkv, proj, qkv, proj, up, down),
            out_specs=(rows, rows, P(), qkv, proj, qkv, proj, up, down),
            check_vma=False,
        )
        return mapped(*args)

    return run
```

```python
from functools import partial
import math

import jax
import jax.numpy as jnp
from jax import lax
from jax.sharding import Mesh, PartitionSpec as P


HD = 64
FRAMES = 8
PATCH = 196


epsilon = 1e-06


def normalize(values, gain_row):
    center = values - jnp.mean(values, axis=-1, keepdims=True)
    spread = jnp.mean(center * center, axis=-1, keepdims=True)
    return center * lax.rsqrt(spread + epsilon) * gain_row


def to_groups(values, temporal):
    trailing = values.shape[1:]
    if temporal:
        clip_count = values.shape[0] // (FRAMES * PATCH)
        shaped = values.reshape((clip_count, FRAMES, PATCH) + trailing)
        shaped = jnp.swapaxes(shaped, 1, 2)
        return shaped.reshape((clip_count * PATCH, FRAMES) + trailing)
    return values.reshape((-1, PATCH) + trailing)


def from_groups(values, temporal):
    trailing = values.shape[2:]
    if temporal:
        clip_count = values.shape[0] // PATCH
        values = jnp.swapaxes(values.reshape((clip_count, PATCH, FRAMES) + trailing), 1, 2)
    return values.reshape((-1,) + trailing)


def attend_forward(normed, w_qkv, temporal):
    factor = 1.0 / math.sqrt(HD)
    width_here = w_qkv.shape[2]
    mixed_qkv = jnp.dot(
        normed, w_qkv.reshape(w_qkv.shape[0], 3 * width_here), preferred_element_type=jnp.float32
    )
    mixed_qkv = mixed_qkv.astype(jnp.bfloat16).reshape(normed.shape[0], 3, width_here // HD, HD)
    grouped = to_groups(mixed_qkv, temporal)
    scores = (
        jnp.einsum(
            "blhe,bmhe->bhlm",
            grouped[:, :, 0],
            grouped[:, :, 1],
            preferred_element_type=jnp.float32,
        )
        * factor
    )
    row_top = jnp.max(scores, axis=-1, keepdims=True)
    shifted = jnp.exp(scores - row_top)
    row_total = jnp.sum(shifted, axis=-1, keepdims=True)
    attn_probs = (shifted / row_total).astype(jnp.bfloat16)
    attended = jnp.einsum(
        "bhlm,bmhe->blhe", attn_probs, grouped[:, :, 2], preferred_element_type=jnp.float32
    )
    merged = from_groups(attended.astype(jnp.bfloat16), temporal).reshape(
        normed.shape[0], width_here
    )
    return (grouped, row_top + jnp.log(row_total), merged)


def attend_backward(normed, w_qkv, w_proj, grouped, summary, merged, grad_rows, temporal):
    factor = 1.0 / math.sqrt(HD)
    width_here = merged.shape[1]
    grad_proj = jnp.dot(grad_rows.T, merged, preferred_element_type=jnp.float32)
    grad_merged = jnp.dot(grad_rows, w_proj.T, preferred_element_type=jnp.float32).astype(
        jnp.bfloat16
    )
    grad_attended = to_groups(grad_merged, temporal)
    grad_attended = grad_attended.reshape(grad_attended.shape[:2] + (width_here // HD, HD))
    query_rows = grouped[:, :, 0]
    key_rows = grouped[:, :, 1]
    value_rows = grouped[:, :, 2]
    scores = (
        jnp.einsum("blhe,bmhe->bhlm", query_rows, key_rows, preferred_element_type=jnp.float32)
        * factor
    )
    attn_probs = jnp.exp(scores - summary)
    grad_value = jnp.einsum(
        "bhlm,blhe->bmhe",
        attn_probs.astype(jnp.bfloat16),
        grad_attended,
        preferred_element_type=jnp.float32,
    )
    grad_probs = jnp.einsum(
        "blhe,bmhe->bhlm", grad_attended, value_rows, preferred_element_type=jnp.float32
    )
    grad_scores = attn_probs * (
        grad_probs - jnp.sum(grad_probs * attn_probs, axis=-1, keepdims=True)
    )
    grad_scores = grad_scores.astype(jnp.bfloat16)
    grad_query = (
        jnp.einsum("bhlm,bmhe->blhe", grad_scores, key_rows, preferred_element_type=jnp.float32)
        * factor
    )
    grad_key = (
        jnp.einsum("bhlm,blhe->bmhe", grad_scores, query_rows, preferred_element_type=jnp.float32)
        * factor
    )
    stacked = jnp.stack([grad_query, grad_key, grad_value], axis=2).astype(jnp.bfloat16)
    grad_mixed = from_groups(stacked, temporal).reshape(normed.shape[0], 3 * width_here)
    grad_qkv = jnp.dot(normed.T, grad_mixed, preferred_element_type=jnp.float32).reshape(
        normed.shape[1], 3, width_here
    )
    grad_normed = jnp.dot(
        grad_mixed,
        w_qkv.reshape(w_qkv.shape[0], 3 * width_here).T,
        preferred_element_type=jnp.float32,
    )
    return (grad_qkv, grad_proj, grad_normed)


def attention_shards(qkv_shard, proj_shard):
    rows, parts, width = qkv_shard.shape
    return jnp.concatenate(
        [qkv_shard.astype(jnp.bfloat16).reshape(rows, parts * width), proj_shard.astype(jnp.bfloat16).T],
        axis=1,
    )


def gather_attention(mine, other, qkv_shape):
    rows, parts, width = qkv_shape
    split = parts * width
    qkv_local = jnp.stack(
        [mine[:, :split].reshape(rows, parts, width), other[:, :split].reshape(rows, parts, width)],
        axis=2,
    ).reshape(rows, 2 * split)
    proj_local = jnp.concatenate([mine[:, split:], other[:, split:]], axis=1)
    full = lax.all_gather(
        jnp.concatenate([qkv_local, proj_local], axis=1), "dp", axis=0, tiled=True
    )
    w_qkv = full[:, : 2 * split].reshape(full.shape[0], parts, 2 * width)
    w_proj = full[:, 2 * split :].T
    return w_qkv, w_proj


def mlp_shards(up_shard, down_shard):
    return jnp.concatenate([up_shard.astype(jnp.bfloat16), down_shard.astype(jnp.bfloat16).T], axis=1)


def gather_mlp(mine, other, width):
    up = lax.all_gather(
        jnp.concatenate([mine[:, :width], other[:, :width]], axis=1), "dp", axis=0, tiled=True
    )
    down = lax.all_gather(
        jnp.concatenate([mine[:, width:], other[:, width:]], axis=1), "dp", axis=0, tiled=True
    )
    return up, down.T


def scatter_rows(pieces):
    flat = [p.reshape(p.shape[0], -1) for p in pieces]
    return lax.psum_scatter(
        jnp.concatenate(flat, axis=1).astype(jnp.bfloat16), "dp", scatter_dimension=0, tiled=True
    )


def finish_attention(local, qkv_shape, proj_shape):
    rows, parts, width = qkv_shape
    split = parts * 2 * width
    qkv = local[:, :split].reshape(rows, parts, 2, width)
    proj = local[:, split:]
    half = proj.shape[1] // 2
    mine = jnp.concatenate([qkv[:, :, 0].reshape(rows, -1), proj[:, :half]], axis=1)
    other = jnp.concatenate([qkv[:, :, 1].reshape(rows, -1), proj[:, half:]], axis=1)
    summed = mine.astype(jnp.float32) + swap_ty(other).astype(jnp.float32)
    return summed[:, : parts * width].reshape(qkv_shape), summed[:, parts * width :].T.reshape(proj_shape)


def finish_mlp(local, up_shape, down_shape):
    width = up_shape[1]
    mine = jnp.concatenate([local[:, :width], local[:, 2 * width : 3 * width]], axis=1)
    other = jnp.concatenate([local[:, width : 2 * width], local[:, 3 * width :]], axis=1)
    summed = mine.astype(jnp.float32) + swap_ty(other).astype(jnp.float32)
    return summed[:, :width].reshape(up_shape), summed[:, width:].T.reshape(down_shape)


def swap_ty(values):
    return lax.ppermute(values, "ty", perm=[(0, 1), (1, 0)])


def per_device(
    tokens,
    cotangent,
    norm_gains,
    qkv_time,
    proj_time,
    qkv_space,
    proj_space,
    up_weight,
    down_weight,
):
    time_mine = attention_shards(qkv_time, proj_time)
    time_qkv, time_proj = gather_attention(time_mine, swap_ty(time_mine), qkv_time.shape)
    later = jnp.concatenate(
        [attention_shards(qkv_space, proj_space), mlp_shards(up_weight, down_weight)], axis=1
    )
    later_other = swap_ty(later)
    cut = later.shape[1] - 2 * up_weight.shape[1]
    space_qkv, space_proj = gather_attention(later[:, :cut], later_other[:, :cut], qkv_space.shape)
    up_full, down_full = gather_mlp(later[:, cut:], later_other[:, cut:], up_weight.shape[1])

    def swap(values):
        return lax.ppermute(values, "core", perm=[(0, 1), (1, 0)])

    def spread_rows(values):
        return jnp.concatenate([values, swap(values)], axis=0)

    def sum_rows(values):
        half = values.shape[0] // 2
        return values[:half] + swap(values[half:].astype(jnp.bfloat16)).astype(jnp.float32)

    spread_grads = spread_rows
    sum_grads = sum_rows

    inputs = tokens.astype(jnp.float32)
    normed_time = spread_rows(normalize(inputs, norm_gains[0]).astype(jnp.bfloat16))
    grouped_time, summary_time, merged_time = attend_forward(normed_time, time_qkv, True)
    after_time = inputs + sum_rows(
        jnp.dot(merged_time, time_proj, preferred_element_type=jnp.float32)
    )
    normed_space = spread_rows(normalize(after_time, norm_gains[1]).astype(jnp.bfloat16))
    grouped_space, summary_space, merged_space = attend_forward(normed_space, space_qkv, False)
    after_space = after_time + sum_rows(
        jnp.dot(merged_space, space_proj, preferred_element_type=jnp.float32)
    )
    normed_mlp = spread_rows(normalize(after_space, norm_gains[2]).astype(jnp.bfloat16))
    hidden_pre = jnp.dot(normed_mlp, up_full, preferred_element_type=jnp.float32)
    hidden = jax.nn.gelu(hidden_pre, approximate=False).astype(jnp.bfloat16)
    output = (
        after_space + sum_rows(jnp.dot(hidden, down_full, preferred_element_type=jnp.float32))
    ).astype(jnp.bfloat16)

    grad_after = cotangent.astype(jnp.float32)
    down_rows = spread_grads(grad_after.astype(jnp.bfloat16))
    grad_down = jnp.dot(down_rows.T, hidden, preferred_element_type=jnp.float32)
    grad_hidden = jnp.dot(down_rows, down_full.T, preferred_element_type=jnp.float32)
    _, gelu_back = jax.vjp(partial(jax.nn.gelu, approximate=False), hidden_pre)
    grad_pre = gelu_back(grad_hidden)[0].astype(jnp.bfloat16)
    grad_up = jnp.dot(normed_mlp.T, grad_pre, preferred_element_type=jnp.float32)
    mlp_local = scatter_rows((grad_up, grad_down))
    grad_up, grad_down = finish_mlp(mlp_local, up_weight.shape, down_weight.shape)
    _, norm_back = jax.vjp(normalize, after_space, norm_gains[2])
    back_rows, gain_mlp = norm_back(
        sum_grads(jnp.dot(grad_pre, up_full.T, preferred_element_type=jnp.float32))
    )
    grad_after = grad_after + back_rows
    _, norm_back = jax.vjp(normalize, after_time, norm_gains[1])
    space_rows = spread_grads(grad_after.astype(jnp.bfloat16))
    grad_qkv_space, grad_proj_space, grad_normed = attend_backward(
        normed_space,
        space_qkv,
        space_proj,
        grouped_space,
        summary_space,
        merged_space,
        space_rows,
        False,
    )
    space_local = scatter_rows((grad_qkv_space, grad_proj_space))
    grad_qkv_space, grad_proj_space = finish_attention(space_local, qkv_space.shape, proj_space.shape)
    back_rows, gain_space = norm_back(sum_grads(grad_normed))
    grad_after = grad_after + back_rows
    time_rows = spread_grads(grad_after.astype(jnp.bfloat16))
    grad_qkv_time, grad_proj_time, grad_normed = attend_backward(
        normed_time, time_qkv, time_proj, grouped_time, summary_time, merged_time, time_rows, True
    )
    grad_qkv_time, grad_proj_time = finish_attention(
        scatter_rows((grad_qkv_time, grad_proj_time)), qkv_time.shape, proj_time.shape
    )
    _, norm_back = jax.vjp(normalize, inputs, norm_gains[0])
    back_rows, gain_time = norm_back(sum_grads(grad_normed))
    grad_tokens = grad_after + back_rows
    grad_gains = lax.psum(jnp.stack([gain_time, gain_space, gain_mlp]), ("dp", "ty", "core"))
    return (
        output,
        grad_tokens,
        grad_gains,
        grad_qkv_time,
        grad_proj_time,
        grad_qkv_space,
        grad_proj_space,
        grad_up,
        grad_down,
    )


def solution(mesh):
    def run(*args):
        rows_here = args[0].shape[0] // mesh.size
        cores = FRAMES * PATCH // rows_here
        tensor = mesh.shape["tensor"]
        assert tensor % cores == 0
        devices = mesh.devices.reshape(mesh.shape["dp"], tensor // cores, cores)
        chips = Mesh(devices, ("dp", "ty", "core"))
        rows = P(("dp", "ty", "core"), None)
        qkv = P("dp", None, ("ty", "core"))
        proj = P(("ty", "core"), "dp")
        up = P("dp", ("ty", "core"))
        down = P(("ty", "core"), "dp")
        mapped = jax.shard_map(
            per_device,
            mesh=chips,
            in_specs=(rows, rows, P(), qkv, proj, qkv, proj, up, down),
            out_specs=(rows, rows, P(), qkv, proj, qkv, proj, up, down),
            check_vma=False,
        )
        return mapped(*args)

    return run
```
